32 devices in a mesh: vox: 16 (over z, y, core), star: 2 (over x).
Axes of the slice: x: 2, y: 2, z: 4, core: 2. Of those that a mesh axis runs over, the one named last changes fastest.
Arguments:
- mean_field: float32 [32, 128, 128], P('vox', 'star'), may hold values from -3 to 3
- deviations: float32 [4, 32, 128, 128], P(None, 'vox', 'star'), may hold values from -4 to 4
- stencil: float32 [3, 3], replicated, may hold values from -2 to 2
- vertical_mix: float32 [128, 128], replicated, may hold values from -0.5 to 0.5
- log_mean: float32 [128], replicated, may hold values from -1.6 to -0.4
- responses: bfloat16 [3072, 128, 128], P(('vox', 'star')), may hold values from 0 to 0.015625
- pair_line: int32 [3072], P(('vox', 'star')), may hold values from 0 to 127
- pair_owner: int32 [3072, 1], P(('vox', 'star')), may hold values from 0 to 15; in each aligned block of 96 rows (0 to 95, 96 to 191, ...) at most 12 rows name the same one
- pair_star: int32 [3072], P(('vox', 'star')), may hold values from 0 to 7
- observed: float32 [256, 128], P(('vox', 'star')), may hold values from 0 to 15
- inv_var: float32 [256, 128], P(('vox', 'star')), may hold values from 0.05 to 0.5
Outputs:
- gradient: float32 [32, 128, 128], P('vox', 'star')
- residual_mean: float32 [256, 128], P(('vox', 'star'))
The draws below stay inside these ranges and needn't reach their ends.
Inputs may be any that keep to these rules, and one draw needn't show every extreme that they name: `pair_owner`: among the 96 pairs of one device at most 12 name one owner, a bound that some block reaches.
All inputs are finite; a program needn't handle non-finite values.
Results may differ from the reference program's by a relative error of at most 0.0015.
Values may be sent and summed in bfloat16 or wider, within the bound.
No kernel may reach another device: no remote copies, remote signals or barrier semaphores. Data moves between devices by JAX's collectives and lax.ppermute only.
A program may use at most 64 MiB of HBM per device.

```python
import math
import jax
import jax.numpy as jnp
import numpy as np
from jax import lax

SAMPLES = 4
BLOCK = 128
CX = 2
CY = 64
STARBLK = 8
PAIRS = 96
LINES = 128
CAPACITY = 12
NX = 32
NY = 128
NSB = 256
NPAIRS = 3072
N_VOX = 16
N_STAR = 2


def touch_ends(values, stream_key, low, largest):
    longest = values.shape.index(max(values.shape))
    spots = []
    for shift in (0, 1):
        where = [jax.random.randint(jax.random.fold_in(stream_key, axis), (), 0, length) for axis, length in enumerate(values.shape)]
        where[longest] = (where[longest] + shift) % values.shape[longest]
        spots.append(tuple(where))
    return values.at[spots[0]].set(low).at[spots[1]].set(largest)


def block_scale(key, dims, shards, smallest, high):
    loudness, own = 1.0, jax.random.fold_in(key, 6)
    for position, parts in shards:
        heights = jnp.exp(jax.random.uniform(jax.random.fold_in(own, position), (parts,), jnp.float32, smallest / len(shards), high / len(shards)))
        loudness = loudness * jnp.repeat(heights, dims[position] // parts).reshape([-1 if axis == position else 1 for axis in range(len(dims))])
    return loudness


def assign_block(rng, own, number, rows, number_of, top, reach, slope):
    sequence = jax.random.permutation(rng, number_of)
    crowded, ordinary = load_shares(number_of, rows * top, reach, slope, True), load_shares(number_of, rows * top, reach, slope, False)
    places = jnp.arange(number_of)

    def named(sizes, offset_by):
        used = int((sizes > 0).sum())
        fixed = max(1, used // 4)
        moved = fixed + (places - fixed + offset_by * (used - fixed)) % max(1, number_of - fixed)
        return jnp.zeros((number_of,), jnp.int32).at[sequence[jnp.where(places < fixed, places, moved)]].set(jnp.asarray(sizes, jnp.int32))

    sizes = jnp.where(number % 4 == 0, named(crowded, number // 4), named(ordinary, number - number // 4 - 1))
    mixed = jax.random.permutation(jax.random.fold_in(own, 3), number_of)
    donor, taker = mixed[0:number_of // 2 * 2:2], mixed[1:number_of // 2 * 2:2]
    slack = jnp.minimum(sizes[donor] - 1, reach - sizes[taker]) // 2
    slack = jnp.where((donor == sequence[0]) | (taker == sequence[0]) | (sizes[taker] == 0), 0, jnp.maximum(slack, 0))
    moved = jax.random.randint(jax.random.fold_in(own, 4), (number_of // 2,), 0, 1 << 20) % (slack + 1)
    sizes = sizes.at[donor].add(-moved).at[taker].add(moved)
    items = jnp.searchsorted(jnp.cumsum(sizes), jnp.arange(rows * top), side="right").astype(jnp.int32)
    table = items.reshape(top, rows).T
    table = table[jax.random.permutation(jax.random.fold_in(own, 1), rows)]
    offset_by = jax.random.randint(jax.random.fold_in(own, 2), (rows, 1), 0, top)
    return jnp.take_along_axis(table, (jnp.arange(top)[None, :] + offset_by) % top, axis=1)


def load_shares(number_of, total, reach, lean, full):
    loads = [(1 << 20) // math.isqrt(rank ** lean) + 1 for rank in range(1, number_of + 1)]
    largest = reach if full else min(reach, max(-(-total // number_of), total * loads[0] // sum(loads)))
    least = 1 if total - largest >= number_of - 1 else 0
    counts, spare = [largest] + [least] * (number_of - 1), total - largest - least * (number_of - 1)
    while spare > 0:
        free = [i for i in range(1, number_of) if counts[i] < largest] or [i for i in range(1, number_of) if counts[i] < reach]
        mass, budget = sum([loads[i] for i in free]), spare
        for i in free:
            more = min(reach - counts[i], max(1, budget * loads[i] // mass), spare)
            counts[i] = counts[i] + more
            spare = spare - more
    return np.array(counts)


def gaussian(own_key, shape, width, reach, pieces=(), kind=jnp.bfloat16):
    factor_of = block_scale(own_key, shape, pieces, -0.22, 0.18) if pieces else 1.0
    drawn = jax.random.normal(own_key, shape, jnp.float32) * width * factor_of
    return jnp.minimum(jnp.maximum(drawn, -reach), reach).astype(kind)


def setup_inputs(seed: int = 0) -> dict:
    streams_of = jax.random.split(jax.random.key(seed), 12)
    mean_field = gaussian(streams_of[0], (NX, NY, BLOCK), 0.5, 3.0, ((0, 16), (1, 2)), jnp.float32)
    deviations = gaussian(streams_of[1], (SAMPLES, NX, NY, BLOCK), 0.8, 4.0, ((1, 16), (2, 2)), jnp.float32)
    stencil = gaussian(streams_of[2], (3, 3), 9 ** -0.5, 2.0, (), jnp.float32)
    vertical_mix = gaussian(streams_of[3], (BLOCK, BLOCK), BLOCK ** -0.5, 0.5, (), jnp.float32)
    log_mean = jnp.clip(jax.random.uniform(streams_of[4], (BLOCK,), jnp.float32, -1.6, -0.4), -1.6, -0.4)
    responses = jnp.clip(0.015625 * jax.random.uniform(streams_of[5], (NPAIRS, BLOCK, BLOCK), jnp.float32) ** block_scale(streams_of[5], (NPAIRS, BLOCK, BLOCK), ((0, 32),), -0.2, 0.2), 0.0, 0.015625).astype(jnp.bfloat16)
    pair_line = touch_ends(jax.random.randint(streams_of[6], (NPAIRS,), 0, LINES), jax.random.fold_in(streams_of[6], 1), 0, LINES - 1).astype(jnp.int32)
    pair_owner_keys = jax.random.split(jax.random.fold_in(streams_of[7], 1), NPAIRS // PAIRS)
    pair_owner_turns = jax.random.permutation(jax.random.fold_in(streams_of[7], 3), NPAIRS // PAIRS)
    pair_owner = jax.vmap(lambda own, number: assign_block(jax.random.fold_in(streams_of[7], 2), own, number, PAIRS, N_VOX, 1, CAPACITY, 2))(pair_owner_keys, pair_owner_turns).reshape((NPAIRS, 1))
    pair_star = touch_ends(jax.random.randint(streams_of[8], (NPAIRS,), 0, STARBLK), jax.random.fold_in(streams_of[8], 1), 0, STARBLK - 1).astype(jnp.int32)
    observed = jnp.clip(15.0 * jax.random.uniform(streams_of[9], (NSB, BLOCK), jnp.float32) ** block_scale(streams_of[9], (NSB, BLOCK), ((0, 32),), -0.2, 0.2), 0.0, 15.0)
    inv_var = jnp.clip(jnp.exp(math.log(0.5) - 2.3025851 * jax.random.uniform(streams_of[10], (NSB, BLOCK), jnp.float32) ** block_scale(streams_of[10], (NSB, BLOCK), ((0, 32),), -0.2, 0.2)), 0.05, 0.5)
    return dict(mean_field=mean_field, deviations=deviations, stencil=stencil, vertical_mix=vertical_mix, log_mean=log_mean, responses=responses, pair_line=pair_line, pair_owner=pair_owner, pair_star=pair_star, observed=observed, inv_var=inv_var)


HIGH = lax.Precision.HIGHEST


def smooth_forward(latent, stencil):
    size_x = latent.shape[1]
    size_y = latent.shape[2]
    padded = jnp.pad(latent, ((0, 0), (1, 1), (1, 1), (0, 0)))
    result = jnp.zeros(latent.shape, jnp.float32)
    for offset_x in range(3):
        for offset_y in range(3):
            result = result + stencil[offset_x, offset_y] * padded[:, offset_x:offset_x + size_x, offset_y:offset_y + size_y, :]
    return result


def smooth_adjoint(grad_smooth, stencil):
    size_x = grad_smooth.shape[1]
    size_y = grad_smooth.shape[2]
    padded = jnp.pad(grad_smooth, ((0, 0), (1, 1), (1, 1), (0, 0)))
    result = jnp.zeros(grad_smooth.shape, jnp.float32)
    for offset_x in range(3):
        for offset_y in range(3):
            result = result + stencil[offset_x, offset_y] * padded[:, 2 - offset_x:2 - offset_x + size_x, 2 - offset_y:2 - offset_y + size_y, :]
    return result


def reference(mean_field, deviations, stencil, vertical_mix, log_mean, responses, pair_line, pair_owner, pair_star, observed, inv_var):
    latent = mean_field[None] + deviations
    smoothed = smooth_forward(latent, stencil)
    log_density = jnp.einsum("sxyw,zw->sxyz", smoothed, vertical_mix, precision=HIGH) + log_mean
    density = jnp.exp(log_density)
    density_b = density.astype(jnp.bfloat16)
    devices = N_VOX * N_STAR
    total_blocks = STARBLK * devices
    tiles = responses.reshape(devices, PAIRS, BLOCK, BLOCK)
    lines = pair_line.reshape(devices, PAIRS)
    owners = pair_owner.reshape(devices, PAIRS)
    stars = pair_star.reshape(devices, PAIRS)

    def locate(device):
        vox_index = device // N_STAR
        star_index = device % N_STAR
        line_id = lines[device]
        pos_x = vox_index * CX + line_id // CY
        pos_y = star_index * CY + line_id % CY
        target = (owners[device] * N_STAR + star_index) * STARBLK + stars[device]
        return pos_x.astype(jnp.int32), pos_y.astype(jnp.int32), target.astype(jnp.int32)

    def forward_step(extinction, device):
        pos_x, pos_y, target = locate(device)
        picked = density_b[:, pos_x, pos_y, :].astype(jnp.float32)
        tile = tiles[device].astype(jnp.float32)
        contribution = jnp.einsum("pij,spj->spi", tile, picked)
        return extinction.at[:, target].add(contribution), None

    extinction, unused = lax.scan(forward_step, jnp.zeros((SAMPLES, total_blocks, BLOCK), jnp.float32), jnp.arange(devices, dtype=jnp.int32))
    misfit = inv_var[None] * (extinction - observed[None])
    misfit_b = misfit.astype(jnp.bfloat16)
    residual_mean = jnp.mean(misfit, axis=0)

    def backward_step(adjoint, device):
        pos_x, pos_y, target = locate(device)
        values = misfit_b[:, target].astype(jnp.float32)
        tile = tiles[device].astype(jnp.float32)
        term = jnp.einsum("pij,spi->spj", tile, values)
        return adjoint.at[:, pos_x, pos_y, :].add(term), None

    adjoint, unused = lax.scan(backward_step, jnp.zeros(latent.shape, jnp.float32), jnp.arange(devices, dtype=jnp.int32))
    grad_log = density * adjoint
    grad_smooth = jnp.einsum("sxyz,zw->sxyw", grad_log, vertical_mix, precision=HIGH)
    gradient = jnp.mean(smooth_adjoint(grad_smooth, stencil) + latent, axis=0)
    return gradient, residual_mean
```

```python
import jax
import jax.numpy as jnp
from jax import lax
from jax.sharding import PartitionSpec as P

HIGH = lax.Precision.HIGHEST


def with_halo(cells, sides, width):
    for axis, dim in sides:
        count = lax.axis_size(axis)
        ends = count - 1
        head = lax.slice_in_dim(cells, 0, width, axis=dim)
        tail = lax.slice_in_dim(cells, cells.shape[dim] - width, cells.shape[dim], axis=dim)
        cells = jnp.concatenate(
            [
                lax.ppermute(tail, axis, [(i, (i + 1) % count) for i in range(ends)]),
                cells,
                lax.ppermute(head, axis, [((i + 1) % count, i) for i in range(ends)]),
            ],
            axis=dim,
        )
    return cells


def per_device(
    mean_field,
    deviations,
    stencil,
    vertical_mix,
    log_mean,
    responses,
    pair_line,
    pair_owner,
    pair_star,
    observed,
    inv_var,
):
    samples = deviations.shape[0]
    width_x = deviations.shape[1]
    width_y = deviations.shape[2]
    length = deviations.shape[3]
    pair_count = responses.shape[0]
    block_count = observed.shape[0]
    group_size = lax.axis_size("vox")
    latent = mean_field[None] + deviations
    padded = with_halo(latent, (("vox", 1), ("star", 2)), 1)
    smoothed = jnp.zeros(latent.shape, jnp.float32)
    for offset_x in range(3):
        for offset_y in range(3):
            smoothed = (
                smoothed
                + stencil[offset_x, offset_y]
                * padded[:, offset_x : offset_x + width_x, offset_y : offset_y + width_y, :]
            )
    log_density = jnp.einsum("sxyw,zw->sxyz", smoothed, vertical_mix, precision=HIGH) + log_mean
    density = jnp.exp(log_density)
    density_b = density.astype(jnp.bfloat16).reshape(samples, width_x * width_y, length)
    picked = jnp.take(density_b, pair_line, axis=1)
    contribution = jnp.einsum("pij,spj->psi", responses, picked, preferred_element_type=jnp.float32)
    star_count = observed.shape[0]
    group_blocks = group_size * star_count
    target = pair_owner[:, 0] * star_count + pair_star
    target_onehot = (
        target[:, None] == jnp.arange(group_blocks, dtype=jnp.int32)[None, :]
    ).astype(jnp.float32)
    partial = jnp.einsum("pb,psi->bsi", target_onehot, contribution, precision=HIGH)
    extinction = lax.psum(partial, "vox")
    table = lax.all_gather(jnp.stack([observed, inv_var]), "vox", axis=1, tiled=True)
    misfit = table[1][:, None, :] * (extinction - table[0][:, None, :])
    misfit_b = misfit.astype(jnp.bfloat16)
    own = lax.dynamic_slice_in_dim(misfit, lax.axis_index("vox") * star_count, star_count, axis=0)
    residual_mean = jnp.mean(own, axis=1)
    pair_misfit = jnp.take(misfit_b, target, axis=0)
    pair_adjoint = jnp.einsum(
        "pij,psi->psj", responses, pair_misfit, preferred_element_type=jnp.float32
    )
    line_onehot = (
        pair_line[:, None] == jnp.arange(width_x * width_y, dtype=jnp.int32)[None, :]
    ).astype(jnp.float32)
    adjoint = jnp.einsum("pb,psj->sbj", line_onehot, pair_adjoint, precision=HIGH).reshape(
        samples, width_x, width_y, length
    )
    grad_log = density * adjoint
    grad_smooth = jnp.einsum("sxyz,zw->sxyw", grad_log, vertical_mix, precision=HIGH)
    padded_grad = with_halo(grad_smooth, (("vox", 1), ("star", 2)), 1)
    grad_latent = jnp.zeros(latent.shape, jnp.float32)
    for offset_x in range(3):
        for offset_y in range(3):
            grad_latent = (
                grad_latent
                + stencil[offset_x, offset_y]
                * padded_grad[
                    :,
                    2 - offset_x : 2 - offset_x + width_x,
                    2 - offset_y : 2 - offset_y + width_y,
                    :,
                ]
            )
    gradient = jnp.mean(grad_latent + latent, axis=0)
    return (gradient, residual_mean)


def solution(mesh):
    placed = (
        P("vox", "star", None),
        P(None, "vox", "star", None),
        P(),
        P(),
        P(),
        P(("vox", "star"), None, None),
        P(("vox", "star")),
        P(("vox", "star"), None),
        P(("vox", "star")),
        P(("vox", "star"), None),
        P(("vox", "star"), None),
    )
    return jax.shard_map(
        per_device,
        mesh=mesh,
        in_specs=placed,
        out_specs=(P("vox", "star", None), P(("vox", "star"), None)),
        check_vma=False,
    )
```

```python
import jax
import jax.numpy as jnp
from jax import lax
from jax.sharding import PartitionSpec as P

HIGH = lax.Precision.HIGHEST


def with_halo(cells, sides, width):
    for axis, dim in sides:
        count = lax.axis_size(axis)
        ends = count - 1
        head = lax.slice_in_dim(cells, 0, width, axis=dim)
        tail = lax.slice_in_dim(cells, cells.shape[dim] - width, cells.shape[dim], axis=dim)
        cells = jnp.concatenate(
            [
                lax.ppermute(tail, axis, [(i, (i + 1) % count) for i in range(ends)]),
                cells,
                lax.ppermute(head, axis, [((i + 1) % count, i) for i in range(ends)]),
            ],
            axis=dim,
        )
    return cells


def per_device(
    mean_field,
    deviations,
    stencil,
    vertical_mix,
    log_mean,
    responses,
    pair_line,
    pair_owner,
    pair_star,
    observed,
    inv_var,
):
    samples = deviations.shape[0]
    width_x = deviations.shape[1]
    width_y = deviations.shape[2]
    length = deviations.shape[3]
    pair_count = responses.shape[0]
    block_count = observed.shape[0]
    group_size = lax.axis_size("vox")
    latent = mean_field[None] + deviations
    padded = with_halo(latent, (("vox", 1), ("star", 2)), 1)
    smoothed = jnp.zeros(latent.shape, jnp.float32)
    for offset_x in range(3):
        for offset_y in range(3):
            smoothed = (
                smoothed
                + stencil[offset_x, offset_y]
                * padded[:, offset_x : offset_x + width_x, offset_y : offset_y + width_y, :]
            )
    log_density = jnp.einsum("sxyw,zw->sxyz", smoothed, vertical_mix, precision=HIGH) + log_mean
    density = jnp.exp(log_density)
    density_b = density.astype(jnp.bfloat16).reshape(samples, width_x * width_y, length)
    picked = jnp.take(density_b, pair_line, axis=1)
    contribution = jnp.einsum("pij,spj->psi", responses, picked, preferred_element_type=jnp.float32)
    star_count = observed.shape[0]
    group_blocks = group_size * star_count
    target = pair_owner[:, 0] * star_count + pair_star
    target_onehot = (
        target[:, None] == jnp.arange(group_blocks, dtype=jnp.int32)[None, :]
    ).astype(jnp.float32)
    partial = jnp.einsum("pb,psi->bsi", target_onehot, contribution, precision=HIGH)
    arrived = lax.all_to_all(
        partial.reshape(group_size, star_count, samples, length),
        "vox",
        split_axis=0,
        concat_axis=0,
        tiled=True,
    )
    extinction = jnp.sum(arrived, axis=0)
    misfit = inv_var[:, None, :] * (extinction - observed[:, None, :])
    residual_mean = jnp.mean(misfit, axis=1)
    misfit_b = misfit.astype(jnp.bfloat16)
    spread = jnp.broadcast_to(misfit_b[None], (group_size,) + misfit_b.shape)
    misfit_b = lax.all_to_all(spread, "vox", split_axis=0, concat_axis=0, tiled=True).reshape(
        group_blocks, samples, length
    )
    pair_misfit = jnp.take(misfit_b, target, axis=0)
    pair_adjoint = jnp.einsum(
        "pij,psi->psj", responses, pair_misfit, preferred_element_type=jnp.float32
    )
    line_onehot = (
        pair_line[:, None] == jnp.arange(width_x * width_y, dtype=jnp.int32)[None, :]
    ).astype(jnp.float32)
    adjoint = jnp.einsum("pb,psj->sbj", line_onehot, pair_adjoint, precision=HIGH).reshape(
        samples, width_x, width_y, length
    )
    grad_log = density * adjoint
    grad_smooth = jnp.einsum("sxyz,zw->sxyw", grad_log, vertical_mix, precision=HIGH)
    padded_grad = with_halo(grad_smooth, (("vox", 1), ("star", 2)), 1)
    grad_latent = jnp.zeros(latent.shape, jnp.float32)
    for offset_x in range(3):
        for offset_y in range(3):
            grad_latent = (
                grad_latent
                + stencil[offset_x, offset_y]
                * padded_grad[
                    :,
                    2 - offset_x : 2 - offset_x + width_x,
                    2 - offset_y : 2 - offset_y + width_y,
                    :,
                ]
            )
    gradient = jnp.mean(grad_latent + latent, axis=0)
    return (gradient, residual_mean)


def solution(mesh):
    placed = (
        P("vox", "star", None),
        P(None, "vox", "star", None),
        P(),
        P(),
        P(),
        P(("vox", "star"), None, None),
        P(("vox", "star")),
        P(("vox", "star"), None),
        P(("vox", "star")),
        P(("vox", "star"), None),
        P(("vox", "star"), None),
    )
    return jax.shard_map(
        per_device,
        mesh=mesh,
        in_specs=placed,
        out_specs=(P("vox", "star", None), P(("vox", "star"), None)),
        check_vma=False,
    )
```

```python
import jax
import jax.numpy as jnp
from jax import lax
from jax.sharding import PartitionSpec as P

HIGH = lax.Precision.HIGHEST


def exchange(cells, axis, dim):
    count = lax.axis_size(axis)
    size = cells.shape[dim]
    head = lax.slice_in_dim(cells, 0, 1, axis=dim)
    tail = lax.slice_in_dim(cells, size - 1, size, axis=dim)
    if count == 2:
        index = lax.axis_index(axis)
        incoming = lax.ppermute(jnp.where(index == 0, tail, head), axis, [(0, 1), (1, 0)])
        zero = jnp.zeros_like(incoming)
        below = jnp.where(index == 1, incoming, zero)
        above = jnp.where(index == 0, incoming, zero)
    else:
        below = lax.ppermute(tail, axis, [(i, i + 1) for i in range(count - 1)])
        above = lax.ppermute(head, axis, [(i + 1, i) for i in range(count - 1)])
    return jnp.concatenate([below, cells, above], axis=dim)


def with_halo(cells):
    return exchange(exchange(cells, "vox", 0), "star", 1)


def per_device(
    mean_field,
    deviations,
    stencil,
    vertical_mix,
    log_mean,
    responses,
    pair_line,
    pair_owner,
    pair_star,
    observed,
    inv_var,
):
    samples = deviations.shape[0]
    width_x = deviations.shape[1]
    width_y = deviations.shape[2]
    length = deviations.shape[3]
    group_size = lax.axis_size("vox")
    star_count = observed.shape[0]
    group_blocks = group_size * star_count
    latent = jnp.transpose(mean_field[None] + deviations, (1, 2, 0, 3))
    padded = with_halo(latent)
    smoothed = jnp.zeros(latent.shape, jnp.float32)
    for offset_x in range(3):
        for offset_y in range(3):
            smoothed = (
                smoothed
                + stencil[offset_x, offset_y]
                * padded[offset_x : offset_x + width_x, offset_y : offset_y + width_y]
            )
    log_density = jnp.einsum("xysw,zw->xysz", smoothed, vertical_mix, precision=HIGH) + log_mean
    density = jnp.exp(log_density)
    density_b = density.astype(jnp.bfloat16).reshape(width_x * width_y, samples, length)
    picked = jnp.take(density_b, pair_line, axis=0)
    contribution = jnp.einsum("pij,psj->psi", responses, picked, preferred_element_type=jnp.float32)
    target = pair_owner[:, 0] * star_count + pair_star
    target_onehot = (
        target[:, None] == jnp.arange(group_blocks, dtype=jnp.int32)[None, :]
    ).astype(jnp.float32)
    partial = jnp.einsum("pb,psi->bsi", target_onehot, contribution, precision=HIGH)
    arrived = lax.all_to_all(
        partial.reshape(group_size, star_count, samples, length),
        "vox",
        split_axis=0,
        concat_axis=0,
        tiled=True,
    )
    extinction = jnp.sum(arrived, axis=0)
    misfit = inv_var[:, None, :] * (extinction - observed[:, None, :])
    residual_mean = jnp.mean(misfit, axis=1)
    misfit_b = misfit.astype(jnp.bfloat16)
    spread = jnp.broadcast_to(misfit_b[None], (group_size,) + misfit_b.shape)
    misfit_b = lax.all_to_all(spread, "vox", split_axis=0, concat_axis=0, tiled=True).reshape(
        group_blocks, samples, length
    )
    pair_misfit = jnp.take(misfit_b, target, axis=0)
    pair_adjoint = jnp.einsum(
        "pij,psi->psj", responses, pair_misfit, preferred_element_type=jnp.float32
    )
    line_onehot = (
        pair_line[:, None] == jnp.arange(width_x * width_y, dtype=jnp.int32)[None, :]
    ).astype(jnp.float32)
    adjoint = jnp.einsum("pb,psj->bsj", line_onehot, pair_adjoint, precision=HIGH).reshape(
        width_x, width_y, samples, length
    )
    grad_log = density * adjoint
    grad_smooth = jnp.einsum("xysz,zw->xysw", grad_log, vertical_mix, precision=HIGH)
    padded_grad = with_halo(grad_smooth)
    grad_latent = jnp.zeros(latent.shape, jnp.float32)
    for offset_x in range(3):
        for offset_y in range(3):
            grad_latent = (
                grad_latent
                + stencil[offset_x, offset_y]
                * padded_grad[2 - offset_x : 2 - offset_x + width_x, 2 - offset_y : 2 - offset_y + width_y]
            )
    gradient = jnp.mean(grad_latent + latent, axis=2)
    return (gradient, residual_mean)


def solution(mesh):
    placed = (
        P("vox", "star", None),
        P(None, "vox", "star", None),
        P(),
        P(),
        P(),
        P(("vox", "star"), None, None),
        P(("vox", "star")),
        P(("vox", "star"), None),
        P(("vox", "star")),
        P(("vox", "star"), None),
        P(("vox", "star"), None),
    )
    return jax.shard_map(
        per_device,
        mesh=mesh,
        in_specs=placed,
        out_specs=(P("vox", "star", None), P(("vox", "star"), None)),
        check_vma=False,
    )
```

```python
import jax
import jax.numpy as jnp
from jax import lax
from jax.sharding import PartitionSpec as P

HIGH = lax.Precision.HIGHEST


def exchange(cells, axis, dim):
    count = lax.axis_size(axis)
    size = cells.shape[dim]
    head = lax.slice_in_dim(cells, 0, 1, axis=dim)
    tail = lax.slice_in_dim(cells, size - 1, size, axis=dim)
    if count == 2:
        index = lax.axis_index(axis)
        incoming = lax.ppermute(jnp.where(index == 0, tail, head), axis, [(0, 1), (1, 0)])
        zero = jnp.zeros_like(incoming)
        below = jnp.where(index == 1, incoming, zero)
        above = jnp.where(index == 0, incoming, zero)
    else:
        below = lax.ppermute(tail, axis, [(i, i + 1) for i in range(count - 1)])
        above = lax.ppermute(head, axis, [(i + 1, i) for i in range(count - 1)])
    return jnp.concatenate([below, cells, above], axis=dim)


def with_halo(cells):
    return exchange(exchange(cells, "vox", 0), "star", 1)


def cube_bits(count):
    bits = count.bit_length() - 1
    return bits if (1 << bits) == count and bits > 0 else None


def reduce_scatter(partial, axis):
    count = partial.shape[0]
    bits = cube_bits(count)
    if bits is None:
        arrived = lax.all_to_all(partial, axis, split_axis=0, concat_axis=0, tiled=True)
        return jnp.sum(arrived, axis=0)
    index = lax.axis_index(axis)
    cells = partial.reshape((2,) * bits + partial.shape[1:])
    for bit in range(bits):
        mine = (index >> bit) & 1
        place = bits - 1 - bit
        keep = lax.dynamic_index_in_dim(cells, mine, axis=place, keepdims=False)
        send = lax.dynamic_index_in_dim(cells, 1 - mine, axis=place, keepdims=False)
        cells = keep + lax.ppermute(send, axis, [(i, i ^ (1 << bit)) for i in range(count)])
    return cells


def all_gather(block, axis, count):
    bits = cube_bits(count)
    if bits is None:
        spread = jnp.broadcast_to(block[None], (count,) + block.shape)
        gathered = lax.all_to_all(spread, axis, split_axis=0, concat_axis=0, tiled=True)
        return gathered.reshape((count * block.shape[0],) + block.shape[1:])
    index = lax.axis_index(axis)
    cells = block
    for bit in reversed(range(bits)):
        low = ((index >> bit) & 1) == 0
        other = lax.ppermute(cells, axis, [(i, i ^ (1 << bit)) for i in range(count)])
        place = bits - 1 - bit
        cells = jnp.stack([jnp.where(low, cells, other), jnp.where(low, other, cells)], axis=place)
    return cells.reshape((count * block.shape[0],) + block.shape[1:])


def per_device(
    mean_field,
    deviations,
    stencil,
    vertical_mix,
    log_mean,
    responses,
    pair_line,
    pair_owner,
    pair_star,
    observed,
    inv_var,
):
    samples = deviations.shape[0]
    width_x = deviations.shape[1]
    width_y = deviations.shape[2]
    length = deviations.shape[3]
    group_size = lax.axis_size("vox")
    star_count = observed.shape[0]
    group_blocks = group_size * star_count
    latent = jnp.transpose(mean_field[None] + deviations, (1, 2, 0, 3))
    padded = with_halo(latent)
    smoothed = jnp.zeros(latent.shape, jnp.float32)
    for offset_x in range(3):
        for offset_y in range(3):
            smoothed = (
                smoothed
                + stencil[offset_x, offset_y]
                * padded[offset_x : offset_x + width_x, offset_y : offset_y + width_y]
            )
    log_density = jnp.einsum("xysw,zw->xysz", smoothed, vertical_mix, precision=HIGH) + log_mean
    density = jnp.exp(log_density)
    density_b = density.astype(jnp.bfloat16).reshape(width_x * width_y, samples, length)
    picked = jnp.take(density_b, pair_line, axis=0)
    contribution = jnp.einsum("pij,psj->psi", responses, picked, preferred_element_type=jnp.float32)
    target = pair_owner[:, 0] * star_count + pair_star
    target_onehot = (
        target[:, None] == jnp.arange(group_blocks, dtype=jnp.int32)[None, :]
    ).astype(jnp.float32)
    partial = jnp.einsum("pb,psi->bsi", target_onehot, contribution, precision=HIGH)
    extinction = reduce_scatter(partial.reshape(group_size, star_count, samples, length), "vox")
    misfit = inv_var[:, None, :] * (extinction - observed[:, None, :])
    residual_mean = jnp.mean(misfit, axis=1)
    misfit_b = all_gather(misfit.astype(jnp.bfloat16), "vox", group_size)
    pair_misfit = jnp.take(misfit_b, target, axis=0)
    pair_adjoint = jnp.einsum(
        "pij,psi->psj", responses, pair_misfit, preferred_element_type=jnp.float32
    )
    line_onehot = (
        pair_line[:, None] == jnp.arange(width_x * width_y, dtype=jnp.int32)[None, :]
    ).astype(jnp.float32)
    adjoint = jnp.einsum("pb,psj->bsj", line_onehot, pair_adjoint, precision=HIGH).reshape(
        width_x, width_y, samples, length
    )
    grad_log = density * adjoint
    grad_smooth = jnp.einsum("xysz,zw->xysw", grad_log, vertical_mix, precision=HIGH)
    padded_grad = with_halo(grad_smooth)
    grad_latent = jnp.zeros(latent.shape, jnp.float32)
    for offset_x in range(3):
        for offset_y in range(3):
            grad_latent = (
                grad_latent
                + stencil[offset_x, offset_y]
                * padded_grad[2 - offset_x : 2 - offset_x + width_x, 2 - offset_y : 2 - offset_y + width_y]
            )
    gradient = jnp.mean(grad_latent + latent, axis=2)
    return (gradient, residual_mean)


def solution(mesh):
    placed = (
        P("vox", "star", None),
        P(None, "vox", "star", None),
        P(),
        P(),
        P(),
        P(("vox", "star"), None, None),
        P(("vox", "star")),
        P(("vox", "star"), None),
        P(("vox", "star")),
        P(("vox", "star"), None),
        P(("vox", "star"), None),
    )
    return jax.shard_map(
        per_device,
        mesh=mesh,
        in_specs=placed,
        out_specs=(P("vox", "star", None), P(("vox", "star"), None)),
        check_vma=False,
    )
```

```python
import jax
import jax.numpy as jnp
from jax import lax
from jax.sharding import PartitionSpec as P

HIGH = lax.Precision.HIGHEST


def edges(cells, axis, dim):
    count = lax.axis_size(axis)
    size = cells.shape[dim]
    head = lax.slice_in_dim(cells, 0, 1, axis=dim)
    tail = lax.slice_in_dim(cells, size - 1, size, axis=dim)
    if count == 2:
        index = lax.axis_index(axis)
        incoming = lax.ppermute(jnp.where(index == 0, tail, head), axis, [(0, 1), (1, 0)])
        zero = jnp.zeros_like(incoming)
        below = jnp.where(index == 1, incoming, zero)
        above = jnp.where(index == 0, incoming, zero)
    else:
        below = lax.ppermute(tail, axis, [(i, i + 1) for i in range(count - 1)])
        above = lax.ppermute(head, axis, [(i + 1, i) for i in range(count - 1)])
    return below, above


def with_halo(cells):
    below, above = edges(cells, "vox", 1)
    extended = jnp.concatenate([below, cells, above], axis=1)
    below, above = edges(extended, "star", 2)
    rows = cells.shape[2]
    spare = -(rows + 2) % 8
    filler = jnp.zeros(extended.shape[:2] + (spare,) + extended.shape[3:], extended.dtype)
    padded = jnp.concatenate([extended, below, above, filler], axis=2)
    return padded.reshape(cells.shape[0], -1, cells.shape[3])


def stencil_matrix(stencil, width_x, width_y, flip):
    rows = width_y + 2 + (-(width_y + 2) % 8)
    out = jnp.arange(width_x * width_y, dtype=jnp.int32)[:, None]
    col = jnp.arange((width_x + 2) * rows, dtype=jnp.int32)[None, :]
    out_x, out_y = out // width_y, out % width_y
    col_x, place = col // rows, col % rows
    col_y = jnp.where(place < width_y, place, jnp.where(place == width_y, -1, width_y))
    if flip:
        shift_x, shift_y = out_x + 2 - col_x, out_y + 1 - col_y
    else:
        shift_x, shift_y = col_x - out_x, col_y - out_y + 1
    live = place < width_y + 2
    matrix = jnp.zeros(shift_x.shape, jnp.float32)
    for a in range(3):
        for b in range(3):
            hit = live & (shift_x == a) & (shift_y == b)
            matrix = matrix + jnp.where(hit, stencil[a, b], 0.0)
    return matrix


def per_device(
    mean_field,
    deviations,
    stencil,
    vertical_mix,
    log_mean,
    responses,
    pair_line,
    pair_owner,
    pair_star,
    observed,
    inv_var,
):
    samples = deviations.shape[0]
    width_x = deviations.shape[1]
    width_y = deviations.shape[2]
    length = deviations.shape[3]
    group_size = lax.axis_size("vox")
    star_count = observed.shape[0]
    group_blocks = group_size * star_count
    latent = mean_field[None] + deviations
    forward = stencil_matrix(stencil, width_x, width_y, False)
    smoothed = jnp.einsum("rc,scz->srz", forward, with_halo(latent), precision=HIGH).reshape(
        latent.shape
    )
    log_density = jnp.einsum("sxyw,zw->sxyz", smoothed, vertical_mix, precision=HIGH) + log_mean
    density = jnp.exp(log_density)
    density_b = density.astype(jnp.bfloat16).reshape(samples, width_x * width_y, length)
    picked = jnp.take(density_b, pair_line, axis=1)
    contribution = jnp.einsum("pij,spj->psi", responses, picked, preferred_element_type=jnp.float32)
    target = pair_owner[:, 0] * star_count + pair_star
    target_onehot = (
        target[:, None] == jnp.arange(group_blocks, dtype=jnp.int32)[None, :]
    ).astype(jnp.float32)
    partial = jnp.einsum("pb,psi->bsi", target_onehot, contribution, precision=HIGH)
    arrived = lax.all_to_all(
        partial.reshape(group_size, star_count, samples, length),
        "vox",
        split_axis=0,
        concat_axis=0,
        tiled=True,
    )
    extinction = jnp.sum(arrived, axis=0)
    misfit = inv_var[:, None, :] * (extinction - observed[:, None, :])
    residual_mean = jnp.mean(misfit, axis=1)
    misfit_b = misfit.astype(jnp.bfloat16)
    spread = jnp.broadcast_to(misfit_b[None], (group_size,) + misfit_b.shape)
    misfit_b = lax.all_to_all(spread, "vox", split_axis=0, concat_axis=0, tiled=True).reshape(
        group_blocks, samples, length
    )
    pair_misfit = jnp.take(misfit_b, target, axis=0)
    pair_adjoint = jnp.einsum(
        "pij,psi->psj", responses, pair_misfit, preferred_element_type=jnp.float32
    )
    line_onehot = (
        pair_line[:, None] == jnp.arange(width_x * width_y, dtype=jnp.int32)[None, :]
    ).astype(jnp.float32)
    adjoint = jnp.einsum("pb,psj->sbj", line_onehot, pair_adjoint, precision=HIGH).reshape(
        samples, width_x, width_y, length
    )
    grad_log = jnp.mean(density * adjoint, axis=0)
    grad_smooth = jnp.einsum("xyz,zw->xyw", grad_log, vertical_mix, precision=HIGH)
    backward = stencil_matrix(stencil, width_x, width_y, True)
    grad_latent = jnp.einsum("rc,scz->srz", backward, with_halo(grad_smooth[None]), precision=HIGH)
    gradient = grad_latent.reshape(width_x, width_y, length) + jnp.mean(latent, axis=0)
    return (gradient, residual_mean)


def solution(mesh):
    placed = (
        P("vox", "star", None),
        P(None, "vox", "star", None),
        P(),
        P(),
        P(),
        P(("vox", "star"), None, None),
        P(("vox", "star")),
        P(("vox", "star"), None),
        P(("vox", "star")),
        P(("vox", "star"), None),
        P(("vox", "star"), None),
    )
    return jax.shard_map(
        per_device,
        mesh=mesh,
        in_specs=placed,
        out_specs=(P("vox", "star", None), P(("vox", "star"), None)),
        check_vma=False,
    )
```

```python
import jax
import jax.numpy as jnp
from jax import lax
from jax.sharding import PartitionSpec as P

HIGH = lax.Precision.HIGHEST


def edges(cells, axis, dim):
    count = lax.axis_size(axis)
    size = cells.shape[dim]
    head = lax.slice_in_dim(cells, 0, 1, axis=dim)
    tail = lax.slice_in_dim(cells, size - 1, size, axis=dim)
    if count == 2:
        index = lax.axis_index(axis)
        incoming = lax.ppermute(jnp.where(index == 0, tail, head), axis, [(0, 1), (1, 0)])
        zero = jnp.zeros_like(incoming)
        below = jnp.where(index == 1, incoming, zero)
        above = jnp.where(index == 0, incoming, zero)
    else:
        below = lax.ppermute(tail, axis, [(i, i + 1) for i in range(count - 1)])
        above = lax.ppermute(head, axis, [(i + 1, i) for i in range(count - 1)])
    return below, above


def with_halo(cells):
    below, above = edges(cells, "vox", 1)
    extended = jnp.concatenate([below, cells, above], axis=1)
    below, above = edges(extended, "star", 2)
    rows = cells.shape[2]
    spare = -(rows + 2) % 8
    filler = jnp.zeros(extended.shape[:2] + (spare,) + extended.shape[3:], extended.dtype)
    padded = jnp.concatenate([extended, below, above, filler], axis=2)
    return padded.reshape(cells.shape[0], -1, cells.shape[3])


def stencil_matrix(stencil, width_x, width_y, flip):
    rows = width_y + 2 + (-(width_y + 2) % 8)
    out = jnp.arange(width_x * width_y, dtype=jnp.int32)[:, None]
    col = jnp.arange((width_x + 2) * rows, dtype=jnp.int32)[None, :]
    out_x, out_y = out // width_y, out % width_y
    col_x, place = col // rows, col % rows
    col_y = jnp.where(place < width_y, place, jnp.where(place == width_y, -1, width_y))
    if flip:
        shift_x, shift_y = out_x + 2 - col_x, out_y + 1 - col_y
    else:
        shift_x, shift_y = col_x - out_x, col_y - out_y + 1
    live = place < width_y + 2
    matrix = jnp.zeros(shift_x.shape, jnp.float32)
    for a in range(3):
        for b in range(3):
            hit = live & (shift_x == a) & (shift_y == b)
            matrix = matrix + jnp.where(hit, stencil[a, b], 0.0)
    return lax.optimization_barrier(matrix)


def per_device(
    mean_field,
    deviations,
    stencil,
    vertical_mix,
    log_mean,
    responses,
    pair_line,
    pair_owner,
    pair_star,
    observed,
    inv_var,
):
    samples = deviations.shape[0]
    width_x = deviations.shape[1]
    width_y = deviations.shape[2]
    length = deviations.shape[3]
    group_size = lax.axis_size("vox")
    star_count = observed.shape[0]
    group_blocks = group_size * star_count
    latent = mean_field[None] + deviations
    forward = stencil_matrix(stencil, width_x, width_y, False)
    smoothed = jnp.einsum("rc,scz->srz", forward, with_halo(latent), precision=HIGH).reshape(
        latent.shape
    )
    log_density = jnp.einsum("sxyw,zw->sxyz", smoothed, vertical_mix, precision=HIGH) + log_mean
    density = jnp.exp(log_density)
    density_b = density.astype(jnp.bfloat16).reshape(samples, width_x * width_y, length)
    picked = jnp.take(density_b, pair_line, axis=1)
    contribution = jnp.einsum("pij,spj->psi", responses, picked, preferred_element_type=jnp.float32)
    target = pair_owner[:, 0] * star_count + pair_star
    target_onehot = (
        target[:, None] == jnp.arange(group_blocks, dtype=jnp.int32)[None, :]
    ).astype(jnp.float32)
    partial = jnp.einsum("pb,psi->bsi", target_onehot, contribution, precision=HIGH)
    arrived = lax.all_to_all(
        partial.reshape(group_size, star_count, samples, length),
        "vox",
        split_axis=0,
        concat_axis=0,
        tiled=True,
    )
    extinction = jnp.sum(arrived, axis=0)
    misfit = inv_var[:, None, :] * (extinction - observed[:, None, :])
    residual_mean = jnp.mean(misfit, axis=1)
    misfit_b = misfit.astype(jnp.bfloat16)
    spread = jnp.broadcast_to(misfit_b[None], (group_size,) + misfit_b.shape)
    misfit_b = lax.all_to_all(spread, "vox", split_axis=0, concat_axis=0, tiled=True).reshape(
        group_blocks, samples, length
    )
    pair_misfit = jnp.take(misfit_b, target, axis=0)
    pair_adjoint = jnp.einsum(
        "pij,psi->psj", responses, pair_misfit, preferred_element_type=jnp.float32
    )
    line_onehot = (
        pair_line[:, None] == jnp.arange(width_x * width_y, dtype=jnp.int32)[None, :]
    ).astype(jnp.float32)
    adjoint = jnp.einsum("pb,psj->sbj", line_onehot, pair_adjoint, precision=HIGH).reshape(
        samples, width_x, width_y, length
    )
    grad_log = jnp.mean(density * adjoint, axis=0)
    grad_smooth = jnp.einsum("xyz,zw->xyw", grad_log, vertical_mix, precision=HIGH)
    backward = stencil_matrix(stencil, width_x, width_y, True)
    grad_latent = jnp.einsum("rc,scz->srz", backward, with_halo(grad_smooth[None]), precision=HIGH)
    gradient = grad_latent.reshape(width_x, width_y, length) + jnp.mean(latent, axis=0)
    return (gradient, residual_mean)


def solution(mesh):
    placed = (
        P("vox", "star", None),
        P(None, "vox", "star", None),
        P(),
        P(),
        P(),
        P(("vox", "star"), None, None),
        P(("vox", "star")),
        P(("vox", "star"), None),
        P(("vox", "star")),
        P(("vox", "star"), None),
        P(("vox", "star"), None),
    )
    return jax.shard_map(
        per_device,
        mesh=mesh,
        in_specs=placed,
        out_specs=(P("vox", "star", None), P(("vox", "star"), None)),
        check_vma=False,
    )
```

```python
import numpy as np
import jax
import jax.numpy as jnp
from jax import lax
from jax.sharding import PartitionSpec as P

HIGH = lax.Precision.HIGHEST


def edges(cells, axis, dim):
    count = lax.axis_size(axis)
    size = cells.shape[dim]
    head = lax.slice_in_dim(cells, 0, 1, axis=dim)
    tail = lax.slice_in_dim(cells, size - 1, size, axis=dim)
    if count == 2:
        index = lax.axis_index(axis)
        incoming = lax.ppermute(jnp.where(index == 0, tail, head), axis, [(0, 1), (1, 0)])
        zero = jnp.zeros_like(incoming)
        below = jnp.where(index == 1, incoming, zero)
        above = jnp.where(index == 0, incoming, zero)
    else:
        below = lax.ppermute(tail, axis, [(i, i + 1) for i in range(count - 1)])
        above = lax.ppermute(head, axis, [(i + 1, i) for i in range(count - 1)])
    return below, above


def with_halo(cells):
    below, above = edges(cells, "vox", 1)
    extended = jnp.concatenate([below, cells, above], axis=1)
    below, above = edges(extended, "star", 2)
    rows = cells.shape[2]
    spare = -(rows + 2) % 8
    filler = jnp.zeros(extended.shape[:2] + (spare,) + extended.shape[3:], extended.dtype)
    padded = jnp.concatenate([extended, below, above, filler], axis=2)
    return padded.reshape(cells.shape[0], -1, cells.shape[3])


def stencil_matrix(stencil, width_x, width_y, flip):
    rows = width_y + 2 + (-(width_y + 2) % 8)
    out = np.arange(width_x * width_y)[:, None]
    col = np.arange((width_x + 2) * rows)[None, :]
    out_x, out_y = out // width_y, out % width_y
    col_x, place = col // rows, col % rows
    col_y = np.where(place < width_y, place, np.where(place == width_y, -1, width_y))
    if flip:
        shift_x, shift_y = out_x + 2 - col_x, out_y + 1 - col_y
    else:
        shift_x, shift_y = col_x - out_x, col_y - out_y + 1
    live = (place < width_y + 2) & (shift_x >= 0) & (shift_x < 3) & (shift_y >= 0) & (shift_y < 3)
    code = jnp.asarray(np.where(live, shift_x * 3 + shift_y, 9).astype(np.int32))
    weights = stencil.reshape(9)
    matrix = jnp.zeros(code.shape, jnp.float32)
    for k in range(9):
        matrix = matrix + jnp.where(code == k, weights[k], 0.0)
    return lax.optimization_barrier(matrix)


def per_device(
    mean_field,
    deviations,
    stencil,
    vertical_mix,
    log_mean,
    responses,
    pair_line,
    pair_owner,
    pair_star,
    observed,
    inv_var,
):
    samples = deviations.shape[0]
    width_x = deviations.shape[1]
    width_y = deviations.shape[2]
    length = deviations.shape[3]
    group_size = lax.axis_size("vox")
    star_count = observed.shape[0]
    group_blocks = group_size * star_count
    latent = mean_field[None] + deviations
    forward = stencil_matrix(stencil, width_x, width_y, False)
    smoothed = jnp.einsum("rc,scz->srz", forward, with_halo(latent), precision=HIGH).reshape(
        latent.shape
    )
    log_density = jnp.einsum("sxyw,zw->sxyz", smoothed, vertical_mix, precision=HIGH) + log_mean
    density = jnp.exp(log_density)
    density_b = density.astype(jnp.bfloat16).reshape(samples, width_x * width_y, length)
    picked = jnp.take(density_b, pair_line, axis=1)
    contribution = jnp.einsum("pij,spj->psi", responses, picked, preferred_element_type=jnp.float32)
    target = pair_owner[:, 0] * star_count + pair_star
    target_onehot = (
        target[:, None] == jnp.arange(group_blocks, dtype=jnp.int32)[None, :]
    ).astype(jnp.float32)
    partial = jnp.einsum("pb,psi->bsi", target_onehot, contribution, precision=HIGH)
    arrived = lax.all_to_all(
        partial.reshape(group_size, star_count, samples, length),
        "vox",
        split_axis=0,
        concat_axis=0,
        tiled=True,
    )
    extinction = jnp.sum(arrived, axis=0)
    misfit = inv_var[:, None, :] * (extinction - observed[:, None, :])
    residual_mean = jnp.mean(misfit, axis=1)
    misfit_b = misfit.astype(jnp.bfloat16)
    spread = jnp.broadcast_to(misfit_b[None], (group_size,) + misfit_b.shape)
    misfit_b = lax.all_to_all(spread, "vox", split_axis=0, concat_axis=0, tiled=True).reshape(
        group_blocks, samples, length
    )
    pair_misfit = jnp.take(misfit_b, target, axis=0)
    pair_adjoint = jnp.einsum(
        "pij,psi->psj", responses, pair_misfit, preferred_element_type=jnp.float32
    )
    line_onehot = (
        pair_line[:, None] == jnp.arange(width_x * width_y, dtype=jnp.int32)[None, :]
    ).astype(jnp.float32)
    adjoint = jnp.einsum("pb,psj->sbj", line_onehot, pair_adjoint, precision=HIGH).reshape(
        samples, width_x, width_y, length
    )
    grad_log = jnp.mean(density * adjoint, axis=0)
    grad_smooth = jnp.einsum("xyz,zw->xyw", grad_log, vertical_mix, precision=HIGH)
    backward = stencil_matrix(stencil, width_x, width_y, True)
    grad_latent = jnp.einsum("rc,scz->srz", backward, with_halo(grad_smooth[None]), precision=HIGH)
    gradient = grad_latent.reshape(width_x, width_y, length) + jnp.mean(latent, axis=0)
    return (gradient, residual_mean)


def solution(mesh):
    placed = (
        P("vox", "star", None),
        P(None, "vox", "star", None),
        P(),
        P(),
        P(),
        P(("vox", "star"), None, None),
        P(("vox", "star")),
        P(("vox", "star"), None),
        P(("vox", "star")),
        P(("vox", "star"), None),
        P(("vox", "star"), None),
    )
    return jax.shard_map(
        per_device,
        mesh=mesh,
        in_specs=placed,
        out_specs=(P("vox", "star", None), P(("vox", "star"), None)),
        check_vma=False,
    )
```

```python
import jax
import jax.numpy as jnp
from jax import lax
from jax.sharding import PartitionSpec as P

HIGH = lax.Precision.HIGHEST


def exchange(cells, axis, dim):
    count = lax.axis_size(axis)
    size = cells.shape[dim]
    head = lax.slice_in_dim(cells, 0, 1, axis=dim)
    tail = lax.slice_in_dim(cells, size - 1, size, axis=dim)
    if count == 2:
        index = lax.axis_index(axis)
        incoming = lax.ppermute(jnp.where(index == 0, tail, head), axis, [(0, 1), (1, 0)])
        zero = jnp.zeros_like(incoming)
        below = jnp.where(index == 1, incoming, zero)
        above = jnp.where(index == 0, incoming, zero)
    else:
        below = lax.ppermute(tail, axis, [(i, i + 1) for i in range(count - 1)])
        above = lax.ppermute(head, axis, [(i + 1, i) for i in range(count - 1)])
    return jnp.concatenate([below, cells, above], axis=dim)


def with_halo(cells):
    return exchange(exchange(cells, "vox", 0), "star", 1)


def per_device(
    mean_field,
    deviations,
    stencil,
    vertical_mix,
    log_mean,
    responses,
    pair_line,
    pair_owner,
    pair_star,
    observed,
    inv_var,
):
    samples = deviations.shape[0]
    width_x = deviations.shape[1]
    width_y = deviations.shape[2]
    length = deviations.shape[3]
    group_size = lax.axis_size("vox")
    star_count = observed.shape[0]
    group_blocks = group_size * star_count
    latent = jnp.transpose(mean_field[None] + deviations, (1, 2, 0, 3))
    padded = with_halo(latent)
    smoothed = jnp.zeros(latent.shape, jnp.float32)
    for offset_x in range(3):
        for offset_y in range(3):
            smoothed = (
                smoothed
                + stencil[offset_x, offset_y]
                * padded[offset_x : offset_x + width_x, offset_y : offset_y + width_y]
            )
    log_density = jnp.einsum("xysw,zw->xysz", smoothed, vertical_mix, precision=HIGH) + log_mean
    density = jnp.exp(log_density)
    density_b = density.astype(jnp.bfloat16).reshape(width_x * width_y, samples, length)
    picked = jnp.take(density_b, pair_line, axis=0)
    contribution = jnp.einsum("pij,psj->psi", responses, picked, preferred_element_type=jnp.float32)
    target = pair_owner[:, 0] * star_count + pair_star
    target_onehot = (
        target[:, None] == jnp.arange(group_blocks, dtype=jnp.int32)[None, :]
    ).astype(jnp.float32)
    partial = jnp.einsum("pb,psi->bsi", target_onehot, contribution, precision=HIGH)
    arrived = lax.all_to_all(
        partial.reshape(group_size, star_count, samples, length),
        "vox",
        split_axis=0,
        concat_axis=0,
        tiled=True,
    )
    extinction = jnp.sum(arrived, axis=0)
    misfit = inv_var[:, None, :] * (extinction - observed[:, None, :])
    residual_mean = jnp.mean(misfit, axis=1)
    misfit_b = misfit.astype(jnp.bfloat16)
    spread = jnp.broadcast_to(misfit_b[None], (group_size,) + misfit_b.shape)
    misfit_b = lax.all_to_all(spread, "vox", split_axis=0, concat_axis=0, tiled=True).reshape(
        group_blocks, samples, length
    )
    pair_misfit = jnp.take(misfit_b, target, axis=0)
    pair_adjoint = jnp.einsum(
        "pij,psi->psj", responses, pair_misfit, preferred_element_type=jnp.float32
    )
    line_onehot = (
        pair_line[:, None] == jnp.arange(width_x * width_y, dtype=jnp.int32)[None, :]
    ).astype(jnp.float32)
    adjoint = jnp.einsum("pb,psj->bsj", line_onehot, pair_adjoint, precision=HIGH).reshape(
        width_x, width_y, samples, length
    )
    grad_log = jnp.mean(density * adjoint, axis=2)
    grad_smooth = jnp.einsum("xyz,zw->xyw", grad_log, vertical_mix, precision=HIGH)
    padded_grad = with_halo(grad_smooth)
    grad_latent = jnp.zeros(grad_smooth.shape, jnp.float32)
    for offset_x in range(3):
        for offset_y in range(3):
            grad_latent = (
                grad_latent
                + stencil[offset_x, offset_y]
                * padded_grad[2 - offset_x : 2 - offset_x + width_x, 2 - offset_y : 2 - offset_y + width_y]
            )
    gradient = grad_latent + jnp.mean(latent, axis=2)
    return (gradient, residual_mean)


def solution(mesh):
    placed = (
        P("vox", "star", None),
        P(None, "vox", "star", None),
        P(),
        P(),
        P(),
        P(("vox", "star"), None, None),
        P(("vox", "star")),
        P(("vox", "star"), None),
        P(("vox", "star")),
        P(("vox", "star"), None),
        P(("vox", "star"), None),
    )
    return jax.shard_map(
        per_device,
        mesh=mesh,
        in_specs=placed,
        out_specs=(P("vox", "star", None), P(("vox", "star"), None)),
        check_vma=False,
    )
```

```python
import jax
import jax.numpy as jnp
from jax import lax
from jax.sharding import PartitionSpec as P

HIGH = lax.Precision.HIGHEST


def exchange(cells, axis, dim):
    count = lax.axis_size(axis)
    size = cells.shape[dim]
    head = lax.slice_in_dim(cells, 0, 1, axis=dim)
    tail = lax.slice_in_dim(cells, size - 1, size, axis=dim)
    if count == 2:
        index = lax.axis_index(axis)
        incoming = lax.ppermute(jnp.where(index == 0, tail, head), axis, [(0, 1), (1, 0)])
        zero = jnp.zeros_like(incoming)
        below = jnp.where(index == 1, incoming, zero)
        above = jnp.where(index == 0, incoming, zero)
    else:
        below = lax.ppermute(tail, axis, [(i, i + 1) for i in range(count - 1)])
        above = lax.ppermute(head, axis, [(i + 1, i) for i in range(count - 1)])
    return jnp.concatenate([below, cells, above], axis=dim)


def with_halo(cells):
    return lax.optimization_barrier(exchange(exchange(cells, "vox", 0), "star", 1))


def per_device(
    mean_field,
    deviations,
    stencil,
    vertical_mix,
    log_mean,
    responses,
    pair_line,
    pair_owner,
    pair_star,
    observed,
    inv_var,
):
    samples = deviations.shape[0]
    width_x = deviations.shape[1]
    width_y = deviations.shape[2]
    length = deviations.shape[3]
    group_size = lax.axis_size("vox")
    star_count = observed.shape[0]
    group_blocks = group_size * star_count
    latent = jnp.transpose(mean_field[None] + deviations, (1, 2, 0, 3))
    padded = with_halo(latent)
    smoothed = jnp.zeros(latent.shape, jnp.float32)
    for offset_x in range(3):
        for offset_y in range(3):
            smoothed = (
                smoothed
                + stencil[offset_x, offset_y]
                * padded[offset_x : offset_x + width_x, offset_y : offset_y + width_y]
            )
    log_density = jnp.einsum("xysw,zw->xysz", smoothed, vertical_mix, precision=HIGH) + log_mean
    density = jnp.exp(log_density)
    density_b = density.astype(jnp.bfloat16).reshape(width_x * width_y, samples, length)
    picked = jnp.take(density_b, pair_line, axis=0)
    contribution = jnp.einsum("pij,psj->psi", responses, picked, preferred_element_type=jnp.float32)
    target = pair_owner[:, 0] * star_count + pair_star
    target_onehot = (
        target[:, None] == jnp.arange(group_blocks, dtype=jnp.int32)[None, :]
    ).astype(jnp.float32)
    partial = jnp.einsum("pb,psi->bsi", target_onehot, contribution, precision=HIGH)
    arrived = lax.all_to_all(
        partial.reshape(group_size, star_count, samples, length),
        "vox",
        split_axis=0,
        concat_axis=0,
        tiled=True,
    )
    extinction = jnp.sum(arrived, axis=0)
    misfit = inv_var[:, None, :] * (extinction - observed[:, None, :])
    residual_mean = jnp.mean(misfit, axis=1)
    misfit_b = misfit.astype(jnp.bfloat16)
    spread = jnp.broadcast_to(misfit_b[None], (group_size,) + misfit_b.shape)
    misfit_b = lax.all_to_all(spread, "vox", split_axis=0, concat_axis=0, tiled=True).reshape(
        group_blocks, samples, length
    )
    pair_misfit = jnp.take(misfit_b, target, axis=0)
    pair_adjoint = jnp.einsum(
        "pij,psi->psj", responses, pair_misfit, preferred_element_type=jnp.float32
    )
    line_onehot = (
        pair_line[:, None] == jnp.arange(width_x * width_y, dtype=jnp.int32)[None, :]
    ).astype(jnp.float32)
    adjoint = jnp.einsum("pb,psj->bsj", line_onehot, pair_adjoint, precision=HIGH).reshape(
        width_x, width_y, samples, length
    )
    grad_log = jnp.mean(density * adjoint, axis=2)
    grad_smooth = jnp.einsum("xyz,zw->xyw", grad_log, vertical_mix, precision=HIGH)
    padded_grad = with_halo(grad_smooth)
    grad_latent = jnp.zeros(grad_smooth.shape, jnp.float32)
    for offset_x in range(3):
        for offset_y in range(3):
            grad_latent = (
                grad_latent
                + stencil[offset_x, offset_y]
                * padded_grad[2 - offset_x : 2 - offset_x + width_x, 2 - offset_y : 2 - offset_y + width_y]
            )
    gradient = grad_latent + jnp.mean(latent, axis=2)
    return (gradient, residual_mean)


def solution(mesh):
    placed = (
        P("vox", "star", None),
        P(None, "vox", "star", None),
        P(),
        P(),
        P(),
        P(("vox", "star"), None, None),
        P(("vox", "star")),
        P(("vox", "star"), None),
        P(("vox", "star")),
        P(("vox", "star"), None),
        P(("vox", "star"), None),
    )
    return jax.shard_map(
        per_device,
        mesh=mesh,
        in_specs=placed,
        out_specs=(P("vox", "star", None), P(("vox", "star"), None)),
        check_vma=False,
    )
```

```python
import jax
import jax.numpy as jnp
from jax import lax
from jax.sharding import PartitionSpec as P

HIGH = lax.Precision.HIGHEST


def exchange(cells, axis, dim):
    count = lax.axis_size(axis)
    size = cells.shape[dim]
    head = lax.slice_in_dim(cells, 0, 1, axis=dim)
    tail = lax.slice_in_dim(cells, size - 1, size, axis=dim)
    if count == 2:
        index = lax.axis_index(axis)
        incoming = lax.ppermute(jnp.where(index == 0, tail, head), axis, [(0, 1), (1, 0)])
        zero = jnp.zeros_like(incoming)
        below = jnp.where(index == 1, incoming, zero)
        above = jnp.where(index == 0, incoming, zero)
    else:
        below = lax.ppermute(tail, axis, [(i, i + 1) for i in range(count - 1)])
        above = lax.ppermute(head, axis, [(i + 1, i) for i in range(count - 1)])
    return jnp.concatenate([below, cells, above], axis=dim)


def with_halo(cells):
    return lax.optimization_barrier(exchange(exchange(cells, "vox", 0), "star", 1))


def per_device(
    mean_field,
    deviations,
    stencil,
    vertical_mix,
    log_mean,
    responses,
    pair_line,
    pair_owner,
    pair_star,
    observed,
    inv_var,
):
    samples = deviations.shape[0]
    width_x = deviations.shape[1]
    width_y = deviations.shape[2]
    length = deviations.shape[3]
    group_size = lax.axis_size("vox")
    star_count = observed.shape[0]
    group_blocks = group_size * star_count
    latent = jnp.transpose(mean_field[None] + deviations, (1, 2, 0, 3))
    weights = lax.optimization_barrier(
        jnp.broadcast_to(stencil.reshape(9, 1), (9, length))
    )
    padded = with_halo(latent)
    smoothed = jnp.zeros(latent.shape, jnp.float32)
    for offset_x in range(3):
        for offset_y in range(3):
            smoothed = (
                smoothed
                + weights[offset_x * 3 + offset_y]
                * padded[offset_x : offset_x + width_x, offset_y : offset_y + width_y]
            )
    log_density = jnp.einsum("xysw,zw->xysz", smoothed, vertical_mix, precision=HIGH) + log_mean
    density = jnp.exp(log_density)
    density_b = density.astype(jnp.bfloat16).reshape(width_x * width_y, samples, length)
    picked = jnp.take(density_b, pair_line, axis=0)
    contribution = jnp.einsum("pij,psj->psi", responses, picked, preferred_element_type=jnp.float32)
    target = pair_owner[:, 0] * star_count + pair_star
    target_onehot = (
        target[:, None] == jnp.arange(group_blocks, dtype=jnp.int32)[None, :]
    ).astype(jnp.float32)
    partial = jnp.einsum("pb,psi->bsi", target_onehot, contribution, precision=HIGH)
    arrived = lax.all_to_all(
        partial.reshape(group_size, star_count, samples, length),
        "vox",
        split_axis=0,
        concat_axis=0,
        tiled=True,
    )
    extinction = jnp.sum(arrived, axis=0)
    misfit = inv_var[:, None, :] * (extinction - observed[:, None, :])
    residual_mean = jnp.mean(misfit, axis=1)
    misfit_b = misfit.astype(jnp.bfloat16)
    spread = jnp.broadcast_to(misfit_b[None], (group_size,) + misfit_b.shape)
    misfit_b = lax.all_to_all(spread, "vox", split_axis=0, concat_axis=0, tiled=True).reshape(
        group_blocks, samples, length
    )
    pair_misfit = jnp.take(misfit_b, target, axis=0)
    pair_adjoint = jnp.einsum(
        "pij,psi->psj", responses, pair_misfit, preferred_element_type=jnp.float32
    )
    line_onehot = (
        pair_line[:, None] == jnp.arange(width_x * width_y, dtype=jnp.int32)[None, :]
    ).astype(jnp.float32)
    adjoint = jnp.einsum("pb,psj->bsj", line_onehot, pair_adjoint, precision=HIGH).reshape(
        width_x, width_y, samples, length
    )
    grad_log = jnp.mean(density * adjoint, axis=2)
    grad_smooth = jnp.einsum("xyz,zw->xyw", grad_log, vertical_mix, precision=HIGH)
    padded_grad = with_halo(grad_smooth)
    grad_latent = jnp.zeros(grad_smooth.shape, jnp.float32)
    for offset_x in range(3):
        for offset_y in range(3):
            grad_latent = (
                grad_latent
                + weights[offset_x * 3 + offset_y]
                * padded_grad[2 - offset_x : 2 - offset_x + width_x, 2 - offset_y : 2 - offset_y + width_y]
            )
    gradient = grad_latent + jnp.mean(latent, axis=2)
    return (gradient, residual_mean)


def solution(mesh):
    placed = (
        P("vox", "star", None),
        P(None, "vox", "star", None),
        P(),
        P(),
        P(),
        P(("vox", "star"), None, None),
        P(("vox", "star")),
        P(("vox", "star"), None),
        P(("vox", "star")),
        P(("vox", "star"), None),
        P(("vox", "star"), None),
    )
    return jax.shard_map(
        per_device,
        mesh=mesh,
        in_specs=placed,
        out_specs=(P("vox", "star", None), P(("vox", "star"), None)),
        check_vma=False,
    )
```

```python
import jax
import jax.numpy as jnp
from jax import lax
from jax.sharding import PartitionSpec as P

HIGH = lax.Precision.HIGHEST


def exchange(cells, axis, dim):
    count = lax.axis_size(axis)
    size = cells.shape[dim]
    head = lax.slice_in_dim(cells, 0, 1, axis=dim)
    tail = lax.slice_in_dim(cells, size - 1, size, axis=dim)
    if count == 2:
        index = lax.axis_index(axis)
        incoming = lax.ppermute(jnp.where(index == 0, tail, head), axis, [(0, 1), (1, 0)])
        zero = jnp.zeros_like(incoming)
        below = jnp.where(index == 1, incoming, zero)
        above = jnp.where(index == 0, incoming, zero)
    else:
        below = lax.ppermute(tail, axis, [(i, i + 1) for i in range(count - 1)])
        above = lax.ppermute(head, axis, [(i + 1, i) for i in range(count - 1)])
    return jnp.concatenate([below, cells, above], axis=dim)


def with_halo(cells):
    return lax.optimization_barrier(exchange(exchange(cells, "vox", 0), "star", 1))


def rows(table, index, axis):
    numbers = lax.GatherDimensionNumbers(
        offset_dims=tuple(d for d in range(table.ndim) if d != axis),
        collapsed_slice_dims=(axis,),
        start_index_map=(axis,),
    )
    sizes = tuple(1 if d == axis else n for d, n in enumerate(table.shape))
    return lax.gather(
        table,
        index[:, None],
        numbers,
        sizes,
        mode=lax.GatherScatterMode.PROMISE_IN_BOUNDS,
    )


def per_device(
    mean_field,
    deviations,
    stencil,
    vertical_mix,
    log_mean,
    responses,
    pair_line,
    pair_owner,
    pair_star,
    observed,
    inv_var,
):
    samples = deviations.shape[0]
    width_x = deviations.shape[1]
    width_y = deviations.shape[2]
    length = deviations.shape[3]
    group_size = lax.axis_size("vox")
    star_count = observed.shape[0]
    group_blocks = group_size * star_count
    latent = jnp.transpose(mean_field[None] + deviations, (1, 2, 0, 3))
    weights = lax.optimization_barrier(
        jnp.broadcast_to(stencil.reshape(9, 1), (9, length))
    )
    padded = with_halo(latent)
    smoothed = jnp.zeros(latent.shape, jnp.float32)
    for offset_x in range(3):
        for offset_y in range(3):
            smoothed = (
                smoothed
                + weights[offset_x * 3 + offset_y]
                * padded[offset_x : offset_x + width_x, offset_y : offset_y + width_y]
            )
    log_density = jnp.einsum("xysw,zw->xysz", smoothed, vertical_mix, precision=HIGH) + log_mean
    density = jnp.exp(log_density)
    density_b = density.astype(jnp.bfloat16).reshape(width_x * width_y, samples, length)
    picked = rows(density_b, pair_line, 0)
    contribution = jnp.einsum("pij,psj->psi", responses, picked, preferred_element_type=jnp.float32)
    target = pair_owner[:, 0] * star_count + pair_star
    target_onehot = (
        target[:, None] == jnp.arange(group_blocks, dtype=jnp.int32)[None, :]
    ).astype(jnp.float32)
    partial = jnp.einsum("pb,psi->bsi", target_onehot, contribution, precision=HIGH)
    arrived = lax.all_to_all(
        partial.reshape(group_size, star_count, samples, length),
        "vox",
        split_axis=0,
        concat_axis=0,
        tiled=True,
    )
    extinction = jnp.sum(arrived, axis=0)
    misfit = inv_var[:, None, :] * (extinction - observed[:, None, :])
    residual_mean = jnp.mean(misfit, axis=1)
    misfit_b = misfit.astype(jnp.bfloat16)
    spread = jnp.broadcast_to(misfit_b[None], (group_size,) + misfit_b.shape)
    misfit_b = lax.all_to_all(spread, "vox", split_axis=0, concat_axis=0, tiled=True).reshape(
        group_blocks, samples, length
    )
    pair_misfit = rows(misfit_b, target, 0)
    pair_adjoint = jnp.einsum(
        "pij,psi->psj", responses, pair_misfit, preferred_element_type=jnp.float32
    )
    line_onehot = (
        pair_line[:, None] == jnp.arange(width_x * width_y, dtype=jnp.int32)[None, :]
    ).astype(jnp.float32)
    adjoint = jnp.einsum("pb,psj->bsj", line_onehot, pair_adjoint, precision=HIGH).reshape(
        width_x, width_y, samples, length
    )
    grad_log = jnp.mean(density * adjoint, axis=2)
    grad_smooth = jnp.einsum("xyz,zw->xyw", grad_log, vertical_mix, precision=HIGH)
    padded_grad = with_halo(grad_smooth)
    grad_latent = jnp.zeros(grad_smooth.shape, jnp.float32)
    for offset_x in range(3):
        for offset_y in range(3):
            grad_latent = (
                grad_latent
                + weights[offset_x * 3 + offset_y]
                * padded_grad[2 - offset_x : 2 - offset_x + width_x, 2 - offset_y : 2 - offset_y + width_y]
            )
    gradient = grad_latent + jnp.mean(latent, axis=2)
    return (gradient, residual_mean)


def solution(mesh):
    placed = (
        P("vox", "star", None),
        P(None, "vox", "star", None),
        P(),
        P(),
        P(),
        P(("vox", "star"), None, None),
        P(("vox", "star")),
        P(("vox", "star"), None),
        P(("vox", "star")),
        P(("vox", "star"), None),
        P(("vox", "star"), None),
    )
    return jax.shard_map(
        per_device,
        mesh=mesh,
        in_specs=placed,
        out_specs=(P("vox", "star", None), P(("vox", "star"), None)),
        check_vma=False,
    )
```

```python
import jax
import jax.numpy as jnp
from jax import lax
from jax.sharding import PartitionSpec as P

HIGH = lax.Precision.HIGHEST


def exchange(cells, axis, dim):
    count = lax.axis_size(axis)
    size = cells.shape[dim]
    head = lax.slice_in_dim(cells, 0, 1, axis=dim)
    tail = lax.slice_in_dim(cells, size - 1, size, axis=dim)
    if count == 2:
        index = lax.axis_index(axis)
        incoming = lax.ppermute(jnp.where(index == 0, tail, head), axis, [(0, 1), (1, 0)])
        zero = jnp.zeros_like(incoming)
        below = jnp.where(index == 1, incoming, zero)
        above = jnp.where(index == 0, incoming, zero)
    else:
        below = lax.ppermute(tail, axis, [(i, i + 1) for i in range(count - 1)])
        above = lax.ppermute(head, axis, [(i + 1, i) for i in range(count - 1)])
    return jnp.concatenate([below, cells, above], axis=dim)


def with_halo(cells):
    return lax.optimization_barrier(exchange(exchange(cells, "vox", 0), "star", 1))


def rows(table, index, axis):
    numbers = lax.GatherDimensionNumbers(
        offset_dims=tuple(d for d in range(table.ndim) if d != axis),
        collapsed_slice_dims=(axis,),
        start_index_map=(axis,),
    )
    sizes = tuple(1 if d == axis else n for d, n in enumerate(table.shape))
    return lax.gather(
        table,
        index[:, None],
        numbers,
        sizes,
        mode=lax.GatherScatterMode.PROMISE_IN_BOUNDS,
    )


def per_device(
    mean_field,
    deviations,
    stencil,
    vertical_mix,
    log_mean,
    responses,
    pair_line,
    pair_owner,
    pair_star,
    observed,
    inv_var,
):
    samples = deviations.shape[0]
    width_x = deviations.shape[1]
    width_y = deviations.shape[2]
    length = deviations.shape[3]
    group_size = lax.axis_size("vox")
    star_count = observed.shape[0]
    group_blocks = group_size * star_count
    latent = jnp.transpose(mean_field[None] + deviations, (1, 2, 0, 3))
    weights = lax.optimization_barrier(
        jnp.broadcast_to(stencil.reshape(9, 1), (9, length))
    )
    padded = with_halo(latent)
    smoothed = jnp.zeros(latent.shape, jnp.float32)
    for offset_x in range(3):
        for offset_y in range(3):
            smoothed = (
                smoothed
                + weights[offset_x * 3 + offset_y]
                * padded[offset_x : offset_x + width_x, offset_y : offset_y + width_y]
            )
    log_density = jnp.einsum("xysw,zw->xysz", smoothed, vertical_mix, precision=HIGH) + log_mean
    density = jnp.exp(log_density)
    density_b = density.astype(jnp.bfloat16).reshape(width_x * width_y, samples, length)
    line_onehot = (
        pair_line[:, None] == jnp.arange(width_x * width_y, dtype=jnp.int32)[None, :]
    ).astype(jnp.float32)
    picked = jnp.einsum(
        "pl,lsz->psz", line_onehot.astype(jnp.bfloat16), density_b, preferred_element_type=jnp.float32
    ).astype(jnp.bfloat16)
    contribution = jnp.einsum("pij,psj->psi", responses, picked, preferred_element_type=jnp.float32)
    target = pair_owner[:, 0] * star_count + pair_star
    target_onehot = (
        target[:, None] == jnp.arange(group_blocks, dtype=jnp.int32)[None, :]
    ).astype(jnp.float32)
    partial = jnp.einsum("pb,psi->bsi", target_onehot, contribution, precision=HIGH)
    arrived = lax.all_to_all(
        partial.reshape(group_size, star_count, samples, length),
        "vox",
        split_axis=0,
        concat_axis=0,
        tiled=True,
    )
    extinction = jnp.sum(arrived, axis=0)
    misfit = inv_var[:, None, :] * (extinction - observed[:, None, :])
    residual_mean = jnp.mean(misfit, axis=1)
    misfit_b = misfit.astype(jnp.bfloat16)
    spread = jnp.broadcast_to(misfit_b[None], (group_size,) + misfit_b.shape)
    misfit_b = lax.all_to_all(spread, "vox", split_axis=0, concat_axis=0, tiled=True).reshape(
        group_blocks, samples, length
    )
    pair_misfit = jnp.einsum(
        "pb,bsi->psi", target_onehot.astype(jnp.bfloat16), misfit_b, preferred_element_type=jnp.float32
    ).astype(jnp.bfloat16)
    pair_adjoint = jnp.einsum(
        "pij,psi->psj", responses, pair_misfit, preferred_element_type=jnp.float32
    )
    adjoint = jnp.einsum("pb,psj->bsj", line_onehot, pair_adjoint, precision=HIGH).reshape(
        width_x, width_y, samples, length
    )
    grad_log = jnp.mean(density * adjoint, axis=2)
    grad_smooth = jnp.einsum("xyz,zw->xyw", grad_log, vertical_mix, precision=HIGH)
    padded_grad = with_halo(grad_smooth)
    grad_latent = jnp.zeros(grad_smooth.shape, jnp.float32)
    for offset_x in range(3):
        for offset_y in range(3):
            grad_latent = (
                grad_latent
                + weights[offset_x * 3 + offset_y]
                * padded_grad[2 - offset_x : 2 - offset_x + width_x, 2 - offset_y : 2 - offset_y + width_y]
            )
    gradient = grad_latent + jnp.mean(latent, axis=2)
    return (gradient, residual_mean)


def solution(mesh):
    placed = (
        P("vox", "star", None),
        P(None, "vox", "star", None),
        P(),
        P(),
        P(),
        P(("vox", "star"), None, None),
        P(("vox", "star")),
        P(("vox", "star"), None),
        P(("vox", "star")),
        P(("vox", "star"), None),
        P(("vox", "star"), None),
    )
    return jax.shard_map(
        per_device,
        mesh=mesh,
        in_specs=placed,
        out_specs=(P("vox", "star", None), P(("vox", "star"), None)),
        check_vma=False,
    )
```

```python
import jax
import jax.numpy as jnp
from jax import lax
from jax.sharding import PartitionSpec as P

HIGH = lax.Precision.HIGHEST


def exchange(cells, axis, dim):
    count = lax.psum(1, axis)
    size = cells.shape[dim]
    head = lax.slice_in_dim(cells, 0, 1, axis=dim)
    tail = lax.slice_in_dim(cells, size - 1, size, axis=dim)
    if count == 2:
        index = lax.axis_index(axis)
        incoming = lax.ppermute(jnp.where(index == 0, tail, head), axis, [(0, 1), (1, 0)])
        zero = jnp.zeros_like(incoming)
        below = jnp.where(index == 1, incoming, zero)
        above = jnp.where(index == 0, incoming, zero)
    else:
        below = lax.ppermute(tail, axis, [(i, i + 1) for i in range(count - 1)])
        above = lax.ppermute(head, axis, [(i + 1, i) for i in range(count - 1)])
    return jnp.concatenate([below, cells, above], axis=dim)


VOX = ("vh", "vc")


def with_halo(cells):
    return lax.optimization_barrier(exchange(exchange(cells, VOX, 0), "star", 1))


def rows(table, index, axis):
    numbers = lax.GatherDimensionNumbers(
        offset_dims=tuple(d for d in range(table.ndim) if d != axis),
        collapsed_slice_dims=(axis,),
        start_index_map=(axis,),
    )
    sizes = tuple(1 if d == axis else n for d, n in enumerate(table.shape))
    return lax.gather(
        table,
        index[:, None],
        numbers,
        sizes,
        mode=lax.GatherScatterMode.PROMISE_IN_BOUNDS,
    )


def per_device(
    mean_field,
    deviations,
    stencil,
    vertical_mix,
    log_mean,
    responses,
    pair_line,
    pair_owner,
    pair_star,
    observed,
    inv_var,
):
    samples = deviations.shape[0]
    width_x = deviations.shape[1]
    width_y = deviations.shape[2]
    length = deviations.shape[3]
    group_size = lax.psum(1, VOX)
    star_count = observed.shape[0]
    group_blocks = group_size * star_count
    latent = jnp.transpose(mean_field[None] + deviations, (1, 2, 0, 3))
    weights = lax.optimization_barrier(
        jnp.broadcast_to(stencil.reshape(9, 1), (9, length))
    )
    padded = with_halo(latent)
    smoothed = jnp.zeros(latent.shape, jnp.float32)
    for offset_x in range(3):
        for offset_y in range(3):
            smoothed = (
                smoothed
                + weights[offset_x * 3 + offset_y]
                * padded[offset_x : offset_x + width_x, offset_y : offset_y + width_y]
            )
    log_density = jnp.einsum("xysw,zw->xysz", smoothed, vertical_mix, precision=HIGH) + log_mean
    density = jnp.exp(log_density)
    density_b = density.astype(jnp.bfloat16).reshape(width_x * width_y, samples, length)
    line_onehot = (
        pair_line[:, None] == jnp.arange(width_x * width_y, dtype=jnp.int32)[None, :]
    ).astype(jnp.float32)
    picked = jnp.einsum(
        "pl,lsz->psz", line_onehot.astype(jnp.bfloat16), density_b, preferred_element_type=jnp.float32
    ).astype(jnp.bfloat16)
    contribution = jnp.einsum("pij,psj->psi", responses, picked, preferred_element_type=jnp.float32)
    target = pair_owner[:, 0] * star_count + pair_star
    target_onehot = (
        target[:, None] == jnp.arange(group_blocks, dtype=jnp.int32)[None, :]
    ).astype(jnp.float32)
    partial = jnp.einsum("pb,psi->bsi", target_onehot, contribution, precision=HIGH)
    pair_size = lax.psum(1, "vc")
    core = lax.axis_index("vc")
    halves = partial.reshape(group_size // pair_size, pair_size, star_count, samples, length)
    keep = lax.dynamic_index_in_dim(halves, core, axis=1, keepdims=False)
    send = lax.dynamic_index_in_dim(halves, 1 - core, axis=1, keepdims=False)
    merged = keep + lax.ppermute(send, "vc", [(0, 1), (1, 0)])
    arrived = lax.all_to_all(merged, "vh", split_axis=0, concat_axis=0, tiled=True)
    extinction = jnp.sum(arrived, axis=0)
    misfit = inv_var[:, None, :] * (extinction - observed[:, None, :])
    residual_mean = jnp.mean(misfit, axis=1)
    misfit_b = misfit.astype(jnp.bfloat16)
    spread = jnp.broadcast_to(misfit_b[None], (group_size,) + misfit_b.shape)
    misfit_b = lax.all_to_all(spread, VOX, split_axis=0, concat_axis=0, tiled=True).reshape(
        group_blocks, samples, length
    )
    pair_misfit = jnp.einsum(
        "pb,bsi->psi", target_onehot.astype(jnp.bfloat16), misfit_b, preferred_element_type=jnp.float32
    ).astype(jnp.bfloat16)
    pair_adjoint = jnp.einsum(
        "pij,psi->psj", responses, pair_misfit, preferred_element_type=jnp.float32
    )
    adjoint = jnp.einsum("pb,psj->bsj", line_onehot, pair_adjoint, precision=HIGH).reshape(
        width_x, width_y, samples, length
    )
    grad_log = jnp.mean(density * adjoint, axis=2)
    grad_smooth = jnp.einsum("xyz,zw->xyw", grad_log, vertical_mix, precision=HIGH)
    padded_grad = with_halo(grad_smooth)
    grad_latent = jnp.zeros(grad_smooth.shape, jnp.float32)
    for offset_x in range(3):
        for offset_y in range(3):
            grad_latent = (
                grad_latent
                + weights[offset_x * 3 + offset_y]
                * padded_grad[2 - offset_x : 2 - offset_x + width_x, 2 - offset_y : 2 - offset_y + width_y]
            )
    gradient = grad_latent + jnp.mean(latent, axis=2)
    return (gradient, residual_mean)


def solution(mesh):
    shape = mesh.devices.shape
    view = jax.sharding.Mesh(
        mesh.devices.reshape(shape[0] // 2, 2, shape[1]), ("vh", "vc", "star")
    )
    placed = (
        P(VOX, "star", None),
        P(None, VOX, "star", None),
        P(),
        P(),
        P(),
        P((*VOX, "star"), None, None),
        P((*VOX, "star")),
        P((*VOX, "star"), None),
        P((*VOX, "star")),
        P((*VOX, "star"), None),
        P((*VOX, "star"), None),
    )
    return jax.shard_map(
        per_device,
        mesh=view,
        in_specs=placed,
        out_specs=(P(VOX, "star", None), P((*VOX, "star"), None)),
        check_vma=False,
    )
```

```python
import jax
import jax.numpy as jnp
from jax import lax
from jax.sharding import PartitionSpec as P

HIGH = lax.Precision.HIGHEST


def exchange(cells, axis, dim, split=False):
    count = lax.psum(1, axis)
    size = cells.shape[dim]
    head = lax.slice_in_dim(cells, 0, 1, axis=dim)
    tail = lax.slice_in_dim(cells, size - 1, size, axis=dim)
    if count == 2:
        index = lax.axis_index(axis)
        incoming = lax.ppermute(jnp.where(index == 0, tail, head), axis, [(0, 1), (1, 0)])
        zero = jnp.zeros_like(incoming)
        below = jnp.where(index == 1, incoming, zero)
        above = jnp.where(index == 0, incoming, zero)
    else:
        below = lax.ppermute(tail, axis, [(i, i + 1) for i in range(count - 1)])
        above = lax.ppermute(head, axis, [(i + 1, i) for i in range(count - 1)])
    if split:
        return below, above
    return jnp.concatenate([below, cells, above], axis=dim)


VOX = ("vh", "vc")


def with_halo(cells):
    count_x = lax.psum(1, VOX)
    count_y = lax.psum(1, "star")
    width_x, width_y = cells.shape[0], cells.shape[1]
    below_x, above_x = exchange(cells, VOX, 0, split=True)
    below_y, above_y = exchange(cells, "star", 1, split=True)
    every = VOX + ("star",)

    def corner(at_x, at_y):
        return cells[at_x : at_x + 1, at_y : at_y + 1]

    def diagonal(piece, step_x, step_y):
        pairs = [
            (u * count_y + t, (u + step_x) * count_y + t + step_y)
            for u in range(count_x)
            for t in range(count_y)
            if 0 <= u + step_x < count_x and 0 <= t + step_y < count_y
        ]
        return lax.ppermute(piece, every, pairs)

    def crossing(piece, step_x):
        pairs = [
            (u * 2 + t, (u + step_x) * 2 + 1 - t)
            for u in range(count_x)
            for t in range(2)
            if 0 <= u + step_x < count_x
        ]
        return lax.ppermute(piece, every, pairs)

    last_x, last_y = width_x - 1, width_y - 1
    if count_y == 2:
        star = lax.axis_index("star")
        low = star == 0
        from_low_x = crossing(jnp.where(low, corner(last_x, last_y), corner(last_x, 0)), 1)
        from_high_x = crossing(jnp.where(low, corner(0, last_y), corner(0, 0)), -1)
        zero = jnp.zeros_like(from_low_x)
        low_low = jnp.where(low, zero, from_low_x)
        low_high = jnp.where(low, from_low_x, zero)
        high_low = jnp.where(low, zero, from_high_x)
        high_high = jnp.where(low, from_high_x, zero)
    else:
        low_low = diagonal(corner(last_x, last_y), 1, 1)
        low_high = diagonal(corner(last_x, 0), 1, -1)
        high_low = diagonal(corner(0, last_y), -1, 1)
        high_high = diagonal(corner(0, 0), -1, -1)
    padded = jnp.concatenate(
        [
            jnp.concatenate([low_low, below_x, low_high], axis=1),
            jnp.concatenate([below_y, cells, above_y], axis=1),
            jnp.concatenate([high_low, above_x, high_high], axis=1),
        ],
        axis=0,
    )
    return lax.optimization_barrier(padded)


def rows(table, index, axis):
    numbers = lax.GatherDimensionNumbers(
        offset_dims=tuple(d for d in range(table.ndim) if d != axis),
        collapsed_slice_dims=(axis,),
        start_index_map=(axis,),
    )
    sizes = tuple(1 if d == axis else n for d, n in enumerate(table.shape))
    return lax.gather(
        table,
        index[:, None],
        numbers,
        sizes,
        mode=lax.GatherScatterMode.PROMISE_IN_BOUNDS,
    )


def per_device(
    mean_field,
    deviations,
    stencil,
    vertical_mix,
    log_mean,
    responses,
    pair_line,
    pair_owner,
    pair_star,
    observed,
    inv_var,
):
    samples = deviations.shape[0]
    width_x = deviations.shape[1]
    width_y = deviations.shape[2]
    length = deviations.shape[3]
    group_size = lax.psum(1, VOX)
    star_count = observed.shape[0]
    group_blocks = group_size * star_count
    latent = jnp.transpose(mean_field[None] + deviations, (1, 2, 0, 3))
    weights = lax.optimization_barrier(
        jnp.broadcast_to(stencil.reshape(9, 1), (9, length))
    )
    padded = with_halo(latent)
    smoothed = jnp.zeros(latent.shape, jnp.float32)
    for offset_x in range(3):
        for offset_y in range(3):
            smoothed = (
                smoothed
                + weights[offset_x * 3 + offset_y]
                * padded[offset_x : offset_x + width_x, offset_y : offset_y + width_y]
            )
    log_density = jnp.einsum("xysw,zw->xysz", smoothed, vertical_mix, precision=HIGH) + log_mean
    density = jnp.exp(log_density)
    density_b = density.astype(jnp.bfloat16).reshape(width_x * width_y, samples, length)
    line_onehot = (
        pair_line[:, None] == jnp.arange(width_x * width_y, dtype=jnp.int32)[None, :]
    ).astype(jnp.float32)
    picked = jnp.einsum(
        "pl,lsz->psz", line_onehot.astype(jnp.bfloat16), density_b, preferred_element_type=jnp.float32
    ).astype(jnp.bfloat16)
    contribution = jnp.einsum("pij,psj->psi", responses, picked, preferred_element_type=jnp.float32)
    target = pair_owner[:, 0] * star_count + pair_star
    target_onehot = (
        target[:, None] == jnp.arange(group_blocks, dtype=jnp.int32)[None, :]
    ).astype(jnp.float32)
    partial = jnp.einsum("pb,psi->bsi", target_onehot, contribution, precision=HIGH)
    pair_size = lax.psum(1, "vc")
    core = lax.axis_index("vc")
    halves = partial.reshape(group_size // pair_size, pair_size, star_count, samples, length)
    keep = lax.dynamic_index_in_dim(halves, core, axis=1, keepdims=False)
    send = lax.dynamic_index_in_dim(halves, 1 - core, axis=1, keepdims=False)
    merged = keep + lax.ppermute(send, "vc", [(0, 1), (1, 0)])
    arrived = lax.all_to_all(merged, "vh", split_axis=0, concat_axis=0, tiled=True)
    extinction = jnp.sum(arrived, axis=0)
    misfit = inv_var[:, None, :] * (extinction - observed[:, None, :])
    residual_mean = jnp.mean(misfit, axis=1)
    misfit_b = misfit.astype(jnp.bfloat16)
    spread = jnp.broadcast_to(misfit_b[None], (group_size,) + misfit_b.shape)
    misfit_b = lax.all_to_all(spread, VOX, split_axis=0, concat_axis=0, tiled=True).reshape(
        group_blocks, samples, length
    )
    pair_misfit = jnp.einsum(
        "pb,bsi->psi", target_onehot.astype(jnp.bfloat16), misfit_b, preferred_element_type=jnp.float32
    ).astype(jnp.bfloat16)
    pair_adjoint = jnp.einsum(
        "pij,psi->psj", responses, pair_misfit, preferred_element_type=jnp.float32
    )
    adjoint = jnp.einsum("pb,psj->bsj", line_onehot, pair_adjoint, precision=HIGH).reshape(
        width_x, width_y, samples, length
    )
    grad_log = jnp.mean(density * adjoint, axis=2)
    grad_smooth = jnp.einsum("xyz,zw->xyw", grad_log, vertical_mix, precision=HIGH)
    padded_grad = with_halo(grad_smooth)
    grad_latent = jnp.zeros(grad_smooth.shape, jnp.float32)
    for offset_x in range(3):
        for offset_y in range(3):
            grad_latent = (
                grad_latent
                + weights[offset_x * 3 + offset_y]
                * padded_grad[2 - offset_x : 2 - offset_x + width_x, 2 - offset_y : 2 - offset_y + width_y]
            )
    gradient = grad_latent + jnp.mean(latent, axis=2)
    return (gradient, residual_mean)


def solution(mesh):
    shape = mesh.devices.shape
    view = jax.sharding.Mesh(
        mesh.devices.reshape(shape[0] // 2, 2, shape[1]), ("vh", "vc", "star")
    )
    placed = (
        P(VOX, "star", None),
        P(None, VOX, "star", None),
        P(),
        P(),
        P(),
        P((*VOX, "star"), None, None),
        P((*VOX, "star")),
        P((*VOX, "star"), None),
        P((*VOX, "star")),
        P((*VOX, "star"), None),
        P((*VOX, "star"), None),
    )
    return jax.shard_map(
        per_device,
        mesh=view,
        in_specs=placed,
        out_specs=(P(VOX, "star", None), P((*VOX, "star"), None)),
        check_vma=False,
    )
```

```python
import jax
import jax.numpy as jnp
from jax import lax
from jax.sharding import PartitionSpec as P

HIGH = lax.Precision.HIGHEST


def exchange(cells, axis, dim, ends=None):
    count = lax.psum(1, axis)
    size = cells.shape[dim]
    if ends is None:
        head = lax.slice_in_dim(cells, 0, 1, axis=dim)
        tail = lax.slice_in_dim(cells, size - 1, size, axis=dim)
    else:
        head, tail = ends
    if count == 2:
        index = lax.axis_index(axis)
        incoming = lax.ppermute(jnp.where(index == 0, tail, head), axis, [(0, 1), (1, 0)])
        zero = jnp.zeros_like(incoming)
        below = jnp.where(index == 1, incoming, zero)
        above = jnp.where(index == 0, incoming, zero)
    else:
        below = lax.ppermute(tail, axis, [(i, i + 1) for i in range(count - 1)])
        above = lax.ppermute(head, axis, [(i + 1, i) for i in range(count - 1)])
    return jnp.concatenate([below, cells, above], axis=dim)


VOX = ("vh", "vc")


def with_halo(cells, ends=None):
    return lax.optimization_barrier(exchange(exchange(cells, VOX, 0, ends), "star", 1))


def rows(table, index, axis):
    numbers = lax.GatherDimensionNumbers(
        offset_dims=tuple(d for d in range(table.ndim) if d != axis),
        collapsed_slice_dims=(axis,),
        start_index_map=(axis,),
    )
    sizes = tuple(1 if d == axis else n for d, n in enumerate(table.shape))
    return lax.gather(
        table,
        index[:, None],
        numbers,
        sizes,
        mode=lax.GatherScatterMode.PROMISE_IN_BOUNDS,
    )


def per_device(
    mean_field,
    deviations,
    stencil,
    vertical_mix,
    log_mean,
    responses,
    pair_line,
    pair_owner,
    pair_star,
    observed,
    inv_var,
):
    samples = deviations.shape[0]
    width_x = deviations.shape[1]
    width_y = deviations.shape[2]
    length = deviations.shape[3]
    group_size = lax.psum(1, VOX)
    star_count = observed.shape[0]
    group_blocks = group_size * star_count
    latent = jnp.transpose(mean_field[None] + deviations, (1, 2, 0, 3))
    weights = lax.optimization_barrier(
        jnp.broadcast_to(stencil.reshape(9, 1), (9, length))
    )
    edge = [
        jnp.transpose(mean_field[at : at + 1][None] + deviations[:, at : at + 1], (1, 2, 0, 3))
        for at in (0, width_x - 1)
    ]
    padded = with_halo(latent, edge)
    smoothed = jnp.zeros(latent.shape, jnp.float32)
    for offset_x in range(3):
        for offset_y in range(3):
            smoothed = (
                smoothed
                + weights[offset_x * 3 + offset_y]
                * padded[offset_x : offset_x + width_x, offset_y : offset_y + width_y]
            )
    log_density = jnp.einsum("xysw,zw->xysz", smoothed, vertical_mix, precision=HIGH) + log_mean
    density = jnp.exp(log_density)
    density_b = density.astype(jnp.bfloat16).reshape(width_x * width_y, samples, length)
    line_onehot = (
        pair_line[:, None] == jnp.arange(width_x * width_y, dtype=jnp.int32)[None, :]
    ).astype(jnp.float32)
    picked = jnp.einsum(
        "pl,lsz->psz", line_onehot.astype(jnp.bfloat16), density_b, preferred_element_type=jnp.float32
    ).astype(jnp.bfloat16)
    contribution = jnp.einsum("pij,psj->psi", responses, picked, preferred_element_type=jnp.float32)
    target = pair_owner[:, 0] * star_count + pair_star
    target_onehot = (
        target[:, None] == jnp.arange(group_blocks, dtype=jnp.int32)[None, :]
    ).astype(jnp.float32)
    partial = jnp.einsum("pb,psi->bsi", target_onehot, contribution, precision=HIGH)
    pair_size = lax.psum(1, "vc")
    core = lax.axis_index("vc")
    halves = partial.reshape(group_size // pair_size, pair_size, star_count, samples, length)
    keep = lax.dynamic_index_in_dim(halves, core, axis=1, keepdims=False)
    send = lax.dynamic_index_in_dim(halves, 1 - core, axis=1, keepdims=False)
    merged = keep + lax.ppermute(send, "vc", [(0, 1), (1, 0)])
    arrived = lax.all_to_all(merged, "vh", split_axis=0, concat_axis=0, tiled=True)
    extinction = jnp.sum(arrived, axis=0)
    misfit = inv_var[:, None, :] * (extinction - observed[:, None, :])
    residual_mean = jnp.mean(misfit, axis=1)
    misfit_b = misfit.astype(jnp.bfloat16)
    spread = jnp.broadcast_to(misfit_b[None], (group_size,) + misfit_b.shape)
    misfit_b = lax.all_to_all(spread, VOX, split_axis=0, concat_axis=0, tiled=True).reshape(
        group_blocks, samples, length
    )
    pair_misfit = jnp.einsum(
        "pb,bsi->psi", target_onehot.astype(jnp.bfloat16), misfit_b, preferred_element_type=jnp.float32
    ).astype(jnp.bfloat16)
    pair_adjoint = jnp.einsum(
        "pij,psi->psj", responses, pair_misfit, preferred_element_type=jnp.float32
    )
    adjoint = jnp.einsum("pb,psj->bsj", line_onehot, pair_adjoint, precision=HIGH).reshape(
        width_x, width_y, samples, length
    )
    grad_log = jnp.mean(density * adjoint, axis=2)
    grad_smooth = jnp.einsum("xyz,zw->xyw", grad_log, vertical_mix, precision=HIGH)
    padded_grad = with_halo(grad_smooth)
    grad_latent = jnp.zeros(grad_smooth.shape, jnp.float32)
    for offset_x in range(3):
        for offset_y in range(3):
            grad_latent = (
                grad_latent
                + weights[offset_x * 3 + offset_y]
                * padded_grad[2 - offset_x : 2 - offset_x + width_x, 2 - offset_y : 2 - offset_y + width_y]
            )
    gradient = grad_latent + jnp.mean(latent, axis=2)
    return (gradient, residual_mean)


def solution(mesh):
    shape = mesh.devices.shape
    view = jax.sharding.Mesh(
        mesh.devices.reshape(shape[0] // 2, 2, shape[1]), ("vh", "vc", "star")
    )
    placed = (
        P(VOX, "star", None),
        P(None, VOX, "star", None),
        P(),
        P(),
        P(),
        P((*VOX, "star"), None, None),
        P((*VOX, "star")),
        P((*VOX, "star"), None),
        P((*VOX, "star")),
        P((*VOX, "star"), None),
        P((*VOX, "star"), None),
    )
    return jax.shard_map(
        per_device,
        mesh=view,
        in_specs=placed,
        out_specs=(P(VOX, "star", None), P((*VOX, "star"), None)),
        check_vma=False,
    )
```

```python
import jax
import jax.numpy as jnp
from jax import lax
from jax.sharding import PartitionSpec as P

HIGH = lax.Precision.HIGHEST


def exchange(cells, axis, dim):
    count = lax.psum(1, axis)
    size = cells.shape[dim]
    head = lax.slice_in_dim(cells, 0, 1, axis=dim)
    tail = lax.slice_in_dim(cells, size - 1, size, axis=dim)
    if count == 2:
        index = lax.axis_index(axis)
        incoming = lax.ppermute(jnp.where(index == 0, tail, head), axis, [(0, 1), (1, 0)])
        zero = jnp.zeros_like(incoming)
        below = jnp.where(index == 1, incoming, zero)
        above = jnp.where(index == 0, incoming, zero)
    else:
        below = lax.ppermute(tail, axis, [(i, i + 1) for i in range(count - 1)])
        above = lax.ppermute(head, axis, [(i + 1, i) for i in range(count - 1)])
    return jnp.concatenate([below, cells, above], axis=dim)


VOX = ("vh", "vc")


def with_halo(cells, dim):
    return lax.optimization_barrier(exchange(exchange(cells, VOX, dim), "star", dim + 1))


def rows(table, index, axis):
    numbers = lax.GatherDimensionNumbers(
        offset_dims=tuple(d for d in range(table.ndim) if d != axis),
        collapsed_slice_dims=(axis,),
        start_index_map=(axis,),
    )
    sizes = tuple(1 if d == axis else n for d, n in enumerate(table.shape))
    return lax.gather(
        table,
        index[:, None],
        numbers,
        sizes,
        mode=lax.GatherScatterMode.PROMISE_IN_BOUNDS,
    )


def per_device(
    mean_field,
    deviations,
    stencil,
    vertical_mix,
    log_mean,
    responses,
    pair_line,
    pair_owner,
    pair_star,
    observed,
    inv_var,
):
    samples = deviations.shape[0]
    width_x = deviations.shape[1]
    width_y = deviations.shape[2]
    length = deviations.shape[3]
    group_size = lax.psum(1, VOX)
    star_count = observed.shape[0]
    group_blocks = group_size * star_count
    latent = mean_field[None] + deviations
    weights = lax.optimization_barrier(
        jnp.broadcast_to(stencil.reshape(9, 1), (9, length))
    )
    padded = with_halo(latent, 1)
    smoothed = jnp.zeros(latent.shape, jnp.float32)
    for offset_x in range(3):
        for offset_y in range(3):
            smoothed = (
                smoothed
                + weights[offset_x * 3 + offset_y]
                * padded[:, offset_x : offset_x + width_x, offset_y : offset_y + width_y]
            )
    log_density = jnp.einsum("sxyw,zw->sxyz", smoothed, vertical_mix, precision=HIGH) + log_mean
    density = jnp.exp(log_density)
    density_b = density.astype(jnp.bfloat16).reshape(samples, width_x * width_y, length)
    line_onehot = (
        pair_line[:, None] == jnp.arange(width_x * width_y, dtype=jnp.int32)[None, :]
    ).astype(jnp.float32)
    picked = jnp.einsum(
        "pl,slz->psz", line_onehot.astype(jnp.bfloat16), density_b, preferred_element_type=jnp.float32
    ).astype(jnp.bfloat16)
    contribution = jnp.einsum("pij,psj->psi", responses, picked, preferred_element_type=jnp.float32)
    target = pair_owner[:, 0] * star_count + pair_star
    target_onehot = (
        target[:, None] == jnp.arange(group_blocks, dtype=jnp.int32)[None, :]
    ).astype(jnp.float32)
    partial = jnp.einsum("pb,psi->bsi", target_onehot, contribution, precision=HIGH)
    pair_size = lax.psum(1, "vc")
    core = lax.axis_index("vc")
    halves = partial.reshape(group_size // pair_size, pair_size, star_count, samples, length)
    keep = lax.dynamic_index_in_dim(halves, core, axis=1, keepdims=False)
    send = lax.dynamic_index_in_dim(halves, 1 - core, axis=1, keepdims=False)
    merged = keep + lax.ppermute(send, "vc", [(0, 1), (1, 0)])
    arrived = lax.all_to_all(merged, "vh", split_axis=0, concat_axis=0, tiled=True)
    extinction = jnp.sum(arrived, axis=0)
    misfit = inv_var[:, None, :] * (extinction - observed[:, None, :])
    residual_mean = jnp.mean(misfit, axis=1)
    misfit_b = misfit.astype(jnp.bfloat16)
    spread = jnp.broadcast_to(misfit_b[None], (group_size,) + misfit_b.shape)
    misfit_b = lax.all_to_all(spread, VOX, split_axis=0, concat_axis=0, tiled=True).reshape(
        group_blocks, samples, length
    )
    pair_misfit = jnp.einsum(
        "pb,bsi->psi", target_onehot.astype(jnp.bfloat16), misfit_b, preferred_element_type=jnp.float32
    ).astype(jnp.bfloat16)
    pair_adjoint = jnp.einsum(
        "pij,psi->psj", responses, pair_misfit, preferred_element_type=jnp.float32
    )
    adjoint = jnp.einsum("pb,psj->sbj", line_onehot, pair_adjoint, precision=HIGH).reshape(
        samples, width_x, width_y, length
    )
    grad_log = jnp.mean(density * adjoint, axis=0)
    grad_smooth = jnp.einsum("xyz,zw->xyw", grad_log, vertical_mix, precision=HIGH)
    padded_grad = with_halo(grad_smooth, 0)
    grad_latent = jnp.zeros(grad_smooth.shape, jnp.float32)
    for offset_x in range(3):
        for offset_y in range(3):
            grad_latent = (
                grad_latent
                + weights[offset_x * 3 + offset_y]
                * padded_grad[2 - offset_x : 2 - offset_x + width_x, 2 - offset_y : 2 - offset_y + width_y]
            )
    gradient = grad_latent + jnp.mean(latent, axis=0)
    return (gradient, residual_mean)


def solution(mesh):
    shape = mesh.devices.shape
    view = jax.sharding.Mesh(
        mesh.devices.reshape(shape[0] // 2, 2, shape[1]), ("vh", "vc", "star")
    )
    placed = (
        P(VOX, "star", None),
        P(None, VOX, "star", None),
        P(),
        P(),
        P(),
        P((*VOX, "star"), None, None),
        P((*VOX, "star")),
        P((*VOX, "star"), None),
        P((*VOX, "star")),
        P((*VOX, "star"), None),
        P((*VOX, "star"), None),
    )
    return jax.shard_map(
        per_device,
        mesh=view,
        in_specs=placed,
        out_specs=(P(VOX, "star", None), P((*VOX, "star"), None)),
        check_vma=False,
    )
```

```python
import jax
import jax.numpy as jnp
from jax import lax
from jax.sharding import PartitionSpec as P

HIGH = lax.Precision.HIGHEST


def exchange(cells, axis, dim):
    count = lax.psum(1, axis)
    size = cells.shape[dim]
    head = lax.slice_in_dim(cells, 0, 1, axis=dim)
    tail = lax.slice_in_dim(cells, size - 1, size, axis=dim)
    if count == 2:
        index = lax.axis_index(axis)
        incoming = lax.ppermute(jnp.where(index == 0, tail, head), axis, [(0, 1), (1, 0)])
        zero = jnp.zeros_like(incoming)
        below = jnp.where(index == 1, incoming, zero)
        above = jnp.where(index == 0, incoming, zero)
    else:
        below = lax.ppermute(tail, axis, [(i, i + 1) for i in range(count - 1)])
        above = lax.ppermute(head, axis, [(i + 1, i) for i in range(count - 1)])
    return jnp.concatenate([below, cells, above], axis=dim)


VOX = ("vh", "vc")


def with_halo(cells, dim):
    return exchange(exchange(cells, VOX, dim), "star", dim + 1)


def rows(table, index, axis):
    numbers = lax.GatherDimensionNumbers(
        offset_dims=tuple(d for d in range(table.ndim) if d != axis),
        collapsed_slice_dims=(axis,),
        start_index_map=(axis,),
    )
    sizes = tuple(1 if d == axis else n for d, n in enumerate(table.shape))
    return lax.gather(
        table,
        index[:, None],
        numbers,
        sizes,
        mode=lax.GatherScatterMode.PROMISE_IN_BOUNDS,
    )


def per_device(
    mean_field,
    deviations,
    stencil,
    vertical_mix,
    log_mean,
    responses,
    pair_line,
    pair_owner,
    pair_star,
    observed,
    inv_var,
):
    samples = deviations.shape[0]
    width_x = deviations.shape[1]
    width_y = deviations.shape[2]
    length = deviations.shape[3]
    group_size = lax.psum(1, VOX)
    star_count = observed.shape[0]
    group_blocks = group_size * star_count
    latent = mean_field[None] + deviations
    weights = lax.optimization_barrier(
        jnp.broadcast_to(stencil.reshape(9, 1), (9, length))
    )
    padded = with_halo(latent, 1)
    smoothed = jnp.zeros(latent.shape, jnp.float32)
    for offset_x in range(3):
        for offset_y in range(3):
            smoothed = (
                smoothed
                + weights[offset_x * 3 + offset_y]
                * padded[:, offset_x : offset_x + width_x, offset_y : offset_y + width_y]
            )
    log_density = jnp.einsum("sxyw,zw->sxyz", smoothed, vertical_mix, precision=HIGH) + log_mean
    density = jnp.exp(log_density)
    density_b = density.astype(jnp.bfloat16).reshape(samples, width_x * width_y, length)
    line_onehot = (
        pair_line[:, None] == jnp.arange(width_x * width_y, dtype=jnp.int32)[None, :]
    ).astype(jnp.float32)
    picked = jnp.einsum(
        "pl,slz->psz", line_onehot.astype(jnp.bfloat16), density_b, preferred_element_type=jnp.float32
    ).astype(jnp.bfloat16)
    contribution = jnp.einsum("pij,psj->psi", responses, picked, preferred_element_type=jnp.float32)
    target = pair_owner[:, 0] * star_count + pair_star
    target_onehot = (
        target[:, None] == jnp.arange(group_blocks, dtype=jnp.int32)[None, :]
    ).astype(jnp.float32)
    partial = jnp.einsum("pb,psi->bsi", target_onehot, contribution, precision=HIGH)
    pair_size = lax.psum(1, "vc")
    core = lax.axis_index("vc")
    halves = partial.reshape(group_size // pair_size, pair_size, star_count, samples, length)
    keep = lax.dynamic_index_in_dim(halves, core, axis=1, keepdims=False)
    send = lax.dynamic_index_in_dim(halves, 1 - core, axis=1, keepdims=False)
    merged = keep + lax.ppermute(send, "vc", [(0, 1), (1, 0)])
    arrived = lax.all_to_all(merged, "vh", split_axis=0, concat_axis=0, tiled=True)
    extinction = jnp.sum(arrived, axis=0)
    misfit = inv_var[:, None, :] * (extinction - observed[:, None, :])
    residual_mean = jnp.mean(misfit, axis=1)
    misfit_b = misfit.astype(jnp.bfloat16)
    spread = jnp.broadcast_to(misfit_b[None], (group_size,) + misfit_b.shape)
    misfit_b = lax.all_to_all(spread, VOX, split_axis=0, concat_axis=0, tiled=True).reshape(
        group_blocks, samples, length
    )
    pair_misfit = jnp.einsum(
        "pb,bsi->psi", target_onehot.astype(jnp.bfloat16), misfit_b, preferred_element_type=jnp.float32
    ).astype(jnp.bfloat16)
    pair_adjoint = jnp.einsum(
        "pij,psi->psj", responses, pair_misfit, preferred_element_type=jnp.float32
    )
    adjoint = jnp.einsum("pb,psj->sbj", line_onehot, pair_adjoint, precision=HIGH).reshape(
        samples, width_x, width_y, length
    )
    grad_log = jnp.mean(density * adjoint, axis=0)
    grad_smooth = jnp.einsum("xyz,zw->xyw", grad_log, vertical_mix, precision=HIGH)
    padded_grad = with_halo(grad_smooth, 0)
    grad_latent = jnp.zeros(grad_smooth.shape, jnp.float32)
    for offset_x in range(3):
        for offset_y in range(3):
            grad_latent = (
                grad_latent
                + weights[offset_x * 3 + offset_y]
                * padded_grad[2 - offset_x : 2 - offset_x + width_x, 2 - offset_y : 2 - offset_y + width_y]
            )
    gradient = grad_latent + jnp.mean(latent, axis=0)
    return (gradient, residual_mean)


def solution(mesh):
    shape = mesh.devices.shape
    view = jax.sharding.Mesh(
        mesh.devices.reshape(shape[0] // 2, 2, shape[1]), ("vh", "vc", "star")
    )
    placed = (
        P(VOX, "star", None),
        P(None, VOX, "star", None),
        P(),
        P(),
        P(),
        P((*VOX, "star"), None, None),
        P((*VOX, "star")),
        P((*VOX, "star"), None),
        P((*VOX, "star")),
        P((*VOX, "star"), None),
        P((*VOX, "star"), None),
    )
    return jax.shard_map(
        per_device,
        mesh=view,
        in_specs=placed,
        out_specs=(P(VOX, "star", None), P((*VOX, "star"), None)),
        check_vma=False,
    )
```

```python
import jax
import jax.numpy as jnp
from jax import lax
from jax.sharding import PartitionSpec as P

HIGH = lax.Precision.HIGHEST


def exchange(cells, axis, dim, ends=None):
    count = lax.psum(1, axis)
    size = cells.shape[dim]
    if ends is None:
        head = lax.slice_in_dim(cells, 0, 1, axis=dim)
        tail = lax.slice_in_dim(cells, size - 1, size, axis=dim)
    else:
        head, tail = ends
    if count == 2:
        index = lax.axis_index(axis)
        incoming = lax.ppermute(jnp.where(index == 0, tail, head), axis, [(0, 1), (1, 0)])
        zero = jnp.zeros_like(incoming)
        below = jnp.where(index == 1, incoming, zero)
        above = jnp.where(index == 0, incoming, zero)
    else:
        below = lax.ppermute(tail, axis, [(i, i + 1) for i in range(count - 1)])
        above = lax.ppermute(head, axis, [(i + 1, i) for i in range(count - 1)])
    return jnp.concatenate([below, cells, above], axis=dim)


VOX = ("vh", "vc")


def with_halo(cells, dim, ends=None):
    return lax.optimization_barrier(exchange(exchange(cells, VOX, dim, ends), "star", dim + 1))


def rows(table, index, axis):
    numbers = lax.GatherDimensionNumbers(
        offset_dims=tuple(d for d in range(table.ndim) if d != axis),
        collapsed_slice_dims=(axis,),
        start_index_map=(axis,),
    )
    sizes = tuple(1 if d == axis else n for d, n in enumerate(table.shape))
    return lax.gather(
        table,
        index[:, None],
        numbers,
        sizes,
        mode=lax.GatherScatterMode.PROMISE_IN_BOUNDS,
    )


def per_device(
    mean_field,
    deviations,
    stencil,
    vertical_mix,
    log_mean,
    responses,
    pair_line,
    pair_owner,
    pair_star,
    observed,
    inv_var,
):
    samples = deviations.shape[0]
    width_x = deviations.shape[1]
    width_y = deviations.shape[2]
    length = deviations.shape[3]
    group_size = lax.psum(1, VOX)
    star_count = observed.shape[0]
    group_blocks = group_size * star_count
    latent = mean_field[None] + deviations
    weights = lax.optimization_barrier(
        jnp.broadcast_to(stencil.reshape(9, 1), (9, length))
    )
    ends = [mean_field[None, at : at + 1] + deviations[:, at : at + 1] for at in (0, width_x - 1)]
    padded = with_halo(latent, 1, ends)
    smoothed = jnp.zeros(latent.shape, jnp.float32)
    for offset_x in range(3):
        for offset_y in range(3):
            smoothed = (
                smoothed
                + weights[offset_x * 3 + offset_y]
                * padded[:, offset_x : offset_x + width_x, offset_y : offset_y + width_y]
            )
    log_density = jnp.einsum("sxyw,zw->sxyz", smoothed, vertical_mix, precision=HIGH) + log_mean
    density = jnp.exp(log_density)
    density_b = density.astype(jnp.bfloat16).reshape(samples, width_x * width_y, length)
    line_onehot = (
        pair_line[:, None] == jnp.arange(width_x * width_y, dtype=jnp.int32)[None, :]
    ).astype(jnp.float32)
    picked = jnp.einsum(
        "pl,slz->psz", line_onehot.astype(jnp.bfloat16), density_b, preferred_element_type=jnp.float32
    ).astype(jnp.bfloat16)
    contribution = jnp.einsum("pij,psj->psi", responses, picked, preferred_element_type=jnp.float32)
    target = pair_owner[:, 0] * star_count + pair_star
    target_onehot = (
        target[:, None] == jnp.arange(group_blocks, dtype=jnp.int32)[None, :]
    ).astype(jnp.float32)
    partial = jnp.einsum("pb,psi->bsi", target_onehot, contribution, precision=HIGH)
    pair_size = lax.psum(1, "vc")
    core = lax.axis_index("vc")
    halves = partial.reshape(group_size // pair_size, pair_size, star_count, samples, length)
    keep = lax.dynamic_index_in_dim(halves, core, axis=1, keepdims=False)
    send = lax.dynamic_index_in_dim(halves, 1 - core, axis=1, keepdims=False)
    merged = keep + lax.ppermute(send, "vc", [(0, 1), (1, 0)])
    arrived = lax.all_to_all(merged, "vh", split_axis=0, concat_axis=0, tiled=True)
    extinction = jnp.sum(arrived, axis=0)
    misfit = inv_var[:, None, :] * (extinction - observed[:, None, :])
    residual_mean = jnp.mean(misfit, axis=1)
    misfit_b = misfit.astype(jnp.bfloat16)
    spread = jnp.broadcast_to(misfit_b[None], (group_size,) + misfit_b.shape)
    misfit_b = lax.all_to_all(spread, VOX, split_axis=0, concat_axis=0, tiled=True).reshape(
        group_blocks, samples, length
    )
    pair_misfit = jnp.einsum(
        "pb,bsi->psi", target_onehot.astype(jnp.bfloat16), misfit_b, preferred_element_type=jnp.float32
    ).astype(jnp.bfloat16)
    pair_adjoint = jnp.einsum(
        "pij,psi->psj", responses, pair_misfit, preferred_element_type=jnp.float32
    )
    adjoint = jnp.einsum("pb,psj->sbj", line_onehot, pair_adjoint, precision=HIGH).reshape(
        samples, width_x, width_y, length
    )
    grad_log = jnp.mean(density * adjoint, axis=0)
    grad_smooth = jnp.einsum("xyz,zw->xyw", grad_log, vertical_mix, precision=HIGH)
    padded_grad = with_halo(grad_smooth, 0)
    grad_latent = jnp.zeros(grad_smooth.shape, jnp.float32)
    for offset_x in range(3):
        for offset_y in range(3):
            grad_latent = (
                grad_latent
                + weights[offset_x * 3 + offset_y]
                * padded_grad[2 - offset_x : 2 - offset_x + width_x, 2 - offset_y : 2 - offset_y + width_y]
            )
    gradient = grad_latent + jnp.mean(latent, axis=0)
    return (gradient, residual_mean)


def solution(mesh):
    shape = mesh.devices.shape
    view = jax.sharding.Mesh(
        mesh.devices.reshape(shape[0] // 2, 2, shape[1]), ("vh", "vc", "star")
    )
    placed = (
        P(VOX, "star", None),
        P(None, VOX, "star", None),
        P(),
        P(),
        P(),
        P((*VOX, "star"), None, None),
        P((*VOX, "star")),
        P((*VOX, "star"), None),
        P((*VOX, "star")),
        P((*VOX, "star"), None),
        P((*VOX, "star"), None),
    )
    return jax.shard_map(
        per_device,
        mesh=view,
        in_specs=placed,
        out_specs=(P(VOX, "star", None), P((*VOX, "star"), None)),
        check_vma=False,
    )
```

```python
import jax
import jax.numpy as jnp
from jax import lax
from jax.sharding import PartitionSpec as P

HIGH = lax.Precision.HIGHEST


def exchange(cells, axis, dim):
    count = lax.psum(1, axis)
    size = cells.shape[dim]
    head = lax.slice_in_dim(cells, 0, 1, axis=dim)
    tail = lax.slice_in_dim(cells, size - 1, size, axis=dim)
    if count == 2:
        index = lax.axis_index(axis)
        incoming = lax.ppermute(jnp.where(index == 0, tail, head), axis, [(0, 1), (1, 0)])
        zero = jnp.zeros_like(incoming)
        below = jnp.where(index == 1, incoming, zero)
        above = jnp.where(index == 0, incoming, zero)
    else:
        below = lax.ppermute(tail, axis, [(i, i + 1) for i in range(count - 1)])
        above = lax.ppermute(head, axis, [(i + 1, i) for i in range(count - 1)])
    return jnp.concatenate([below, cells, above], axis=dim)


VOX = ("va", "vb", "vc")


def with_halo(cells, dim):
    return lax.optimization_barrier(exchange(exchange(cells, VOX, dim), "star", dim + 1))


def rows(table, index, axis):
    numbers = lax.GatherDimensionNumbers(
        offset_dims=tuple(d for d in range(table.ndim) if d != axis),
        collapsed_slice_dims=(axis,),
        start_index_map=(axis,),
    )
    sizes = tuple(1 if d == axis else n for d, n in enumerate(table.shape))
    return lax.gather(
        table,
        index[:, None],
        numbers,
        sizes,
        mode=lax.GatherScatterMode.PROMISE_IN_BOUNDS,
    )


def per_device(
    mean_field,
    deviations,
    stencil,
    vertical_mix,
    log_mean,
    responses,
    pair_line,
    pair_owner,
    pair_star,
    observed,
    inv_var,
):
    samples = deviations.shape[0]
    width_x = deviations.shape[1]
    width_y = deviations.shape[2]
    length = deviations.shape[3]
    group_size = lax.psum(1, VOX)
    star_count = observed.shape[0]
    group_blocks = group_size * star_count
    latent = mean_field[None] + deviations
    weights = lax.optimization_barrier(
        jnp.broadcast_to(stencil.reshape(9, 1), (9, length))
    )
    padded = with_halo(latent, 1)
    smoothed = jnp.zeros(latent.shape, jnp.float32)
    for offset_x in range(3):
        for offset_y in range(3):
            smoothed = (
                smoothed
                + weights[offset_x * 3 + offset_y]
                * padded[:, offset_x : offset_x + width_x, offset_y : offset_y + width_y]
            )
    log_density = jnp.einsum("sxyw,zw->sxyz", smoothed, vertical_mix, precision=HIGH) + log_mean
    density = jnp.exp(log_density)
    density_b = density.astype(jnp.bfloat16).reshape(samples, width_x * width_y, length)
    line_onehot = (
        pair_line[:, None] == jnp.arange(width_x * width_y, dtype=jnp.int32)[None, :]
    ).astype(jnp.float32)
    picked = jnp.einsum(
        "pl,slz->psz", line_onehot.astype(jnp.bfloat16), density_b, preferred_element_type=jnp.float32
    ).astype(jnp.bfloat16)
    contribution = jnp.einsum("pij,psj->psi", responses, picked, preferred_element_type=jnp.float32)
    target = pair_owner[:, 0] * star_count + pair_star
    target_onehot = (
        target[:, None] == jnp.arange(group_blocks, dtype=jnp.int32)[None, :]
    ).astype(jnp.float32)
    partial = jnp.einsum("pb,psi->bsi", target_onehot, contribution, precision=HIGH)
    merged = partial.reshape(group_size // 4, 2, 2, star_count, samples, length)
    for axis, place in (("vc", 2), ("vb", 1)):
        bit = lax.axis_index(axis)
        keep = lax.dynamic_index_in_dim(merged, bit, axis=place, keepdims=False)
        send = lax.dynamic_index_in_dim(merged, 1 - bit, axis=place, keepdims=False)
        merged = keep + lax.ppermute(send, axis, [(0, 1), (1, 0)])
    arrived = lax.all_to_all(merged, "va", split_axis=0, concat_axis=0, tiled=True)
    extinction = jnp.sum(arrived, axis=0)
    misfit = inv_var[:, None, :] * (extinction - observed[:, None, :])
    residual_mean = jnp.mean(misfit, axis=1)
    misfit_b = misfit.astype(jnp.bfloat16)
    spread = jnp.broadcast_to(misfit_b[None], (group_size,) + misfit_b.shape)
    misfit_b = lax.all_to_all(spread, VOX, split_axis=0, concat_axis=0, tiled=True).reshape(
        group_blocks, samples, length
    )
    pair_misfit = jnp.einsum(
        "pb,bsi->psi", target_onehot.astype(jnp.bfloat16), misfit_b, preferred_element_type=jnp.float32
    ).astype(jnp.bfloat16)
    pair_adjoint = jnp.einsum(
        "pij,psi->psj", responses, pair_misfit, preferred_element_type=jnp.float32
    )
    adjoint = jnp.einsum("pb,psj->sbj", line_onehot, pair_adjoint, precision=HIGH).reshape(
        samples, width_x, width_y, length
    )
    grad_log = jnp.mean(density * adjoint, axis=0)
    grad_smooth = jnp.einsum("xyz,zw->xyw", grad_log, vertical_mix, precision=HIGH)
    padded_grad = with_halo(grad_smooth, 0)
    grad_latent = jnp.zeros(grad_smooth.shape, jnp.float32)
    for offset_x in range(3):
        for offset_y in range(3):
            grad_latent = (
                grad_latent
                + weights[offset_x * 3 + offset_y]
                * padded_grad[2 - offset_x : 2 - offset_x + width_x, 2 - offset_y : 2 - offset_y + width_y]
            )
    gradient = grad_latent + jnp.mean(latent, axis=0)
    return (gradient, residual_mean)


def solution(mesh):
    shape = mesh.devices.shape
    view = jax.sharding.Mesh(
        mesh.devices.reshape(shape[0] // 4, 2, 2, shape[1]), ("va", "vb", "vc", "star")
    )
    placed = (
        P(VOX, "star", None),
        P(None, VOX, "star", None),
        P(),
        P(),
        P(),
        P((*VOX, "star"), None, None),
        P((*VOX, "star")),
        P((*VOX, "star"), None),
        P((*VOX, "star")),
        P((*VOX, "star"), None),
        P((*VOX, "star"), None),
    )
    return jax.shard_map(
        per_device,
        mesh=view,
        in_specs=placed,
        out_specs=(P(VOX, "star", None), P((*VOX, "star"), None)),
        check_vma=False,
    )
```

```python
import jax
import jax.numpy as jnp
from jax import lax
from jax.sharding import PartitionSpec as P

HIGH = lax.Precision.HIGHEST


def exchange(cells, axis, dim):
    count = lax.psum(1, axis)
    size = cells.shape[dim]
    head = lax.slice_in_dim(cells, 0, 1, axis=dim)
    tail = lax.slice_in_dim(cells, size - 1, size, axis=dim)
    if count == 2:
        index = lax.axis_index(axis)
        incoming = lax.ppermute(jnp.where(index == 0, tail, head), axis, [(0, 1), (1, 0)])
        zero = jnp.zeros_like(incoming)
        below = jnp.where(index == 1, incoming, zero)
        above = jnp.where(index == 0, incoming, zero)
    else:
        below = lax.ppermute(tail, axis, [(i, i + 1) for i in range(count - 1)])
        above = lax.ppermute(head, axis, [(i + 1, i) for i in range(count - 1)])
    return jnp.concatenate([below, cells, above], axis=dim)


VOX = ("vh", "vc")


def with_halo(cells, dim):
    return lax.optimization_barrier(exchange(exchange(cells, VOX, dim), "star", dim + 1))


def rows(table, index, axis):
    numbers = lax.GatherDimensionNumbers(
        offset_dims=tuple(d for d in range(table.ndim) if d != axis),
        collapsed_slice_dims=(axis,),
        start_index_map=(axis,),
    )
    sizes = tuple(1 if d == axis else n for d, n in enumerate(table.shape))
    return lax.gather(
        table,
        index[:, None],
        numbers,
        sizes,
        mode=lax.GatherScatterMode.PROMISE_IN_BOUNDS,
    )


def per_device(
    mean_field,
    deviations,
    stencil,
    vertical_mix,
    log_mean,
    responses,
    pair_line,
    pair_owner,
    pair_star,
    observed,
    inv_var,
):
    samples = deviations.shape[0]
    width_x = deviations.shape[1]
    width_y = deviations.shape[2]
    length = deviations.shape[3]
    group_size = lax.psum(1, VOX)
    star_count = observed.shape[0]
    group_blocks = group_size * star_count
    latent = mean_field[None] + deviations
    weights = lax.optimization_barrier(
        jnp.broadcast_to(stencil.reshape(9, 1), (9, length))
    )
    padded = with_halo(latent, 1)
    smoothed = jnp.zeros(latent.shape, jnp.float32)
    for offset_x in range(3):
        for offset_y in range(3):
            smoothed = (
                smoothed
                + weights[offset_x * 3 + offset_y]
                * padded[:, offset_x : offset_x + width_x, offset_y : offset_y + width_y]
            )
    log_density = jnp.einsum("sxyw,zw->sxyz", smoothed, vertical_mix, precision=HIGH) + log_mean
    density = jnp.exp(log_density)
    density_b = density.astype(jnp.bfloat16).reshape(samples, width_x * width_y, length)
    line_onehot = (
        pair_line[:, None] == jnp.arange(width_x * width_y, dtype=jnp.int32)[None, :]
    ).astype(jnp.float32)
    picked = jnp.einsum(
        "pl,slz->psz", line_onehot.astype(jnp.bfloat16), density_b, preferred_element_type=jnp.float32
    ).astype(jnp.bfloat16)
    contribution = jnp.einsum("pij,psj->psi", responses, picked, preferred_element_type=jnp.float32)
    target = pair_owner[:, 0] * star_count + pair_star
    target_onehot = (
        target[:, None] == jnp.arange(group_blocks, dtype=jnp.int32)[None, :]
    ).astype(jnp.float32)
    partial = jnp.einsum("pb,psi->bsi", target_onehot, contribution, precision=HIGH)
    pair_size = lax.psum(1, "vc")
    core = lax.axis_index("vc")
    halves = partial.reshape(group_size // pair_size, pair_size, star_count, samples, length)
    keep = lax.dynamic_index_in_dim(halves, core, axis=1, keepdims=False)
    send = lax.dynamic_index_in_dim(halves, 1 - core, axis=1, keepdims=False)
    merged = keep + lax.ppermute(send, "vc", [(0, 1), (1, 0)])
    arrived = lax.all_to_all(merged, "vh", split_axis=0, concat_axis=0, tiled=True)
    extinction = jnp.sum(arrived, axis=0)
    misfit = inv_var[:, None, :] * (extinction - observed[:, None, :])
    residual_mean = jnp.mean(misfit, axis=1)
    misfit_b = misfit.astype(jnp.bfloat16)
    misfit_b = lax.all_gather(misfit_b, VOX, axis=0, tiled=True)
    pair_misfit = jnp.einsum(
        "pb,bsi->psi", target_onehot.astype(jnp.bfloat16), misfit_b, preferred_element_type=jnp.float32
    ).astype(jnp.bfloat16)
    pair_adjoint = jnp.einsum(
        "pij,psi->psj", responses, pair_misfit, preferred_element_type=jnp.float32
    )
    adjoint = jnp.einsum("pb,psj->sbj", line_onehot, pair_adjoint, precision=HIGH).reshape(
        samples, width_x, width_y, length
    )
    grad_log = jnp.mean(density * adjoint, axis=0)
    grad_smooth = jnp.einsum("xyz,zw->xyw", grad_log, vertical_mix, precision=HIGH)
    padded_grad = with_halo(grad_smooth, 0)
    grad_latent = jnp.zeros(grad_smooth.shape, jnp.float32)
    for offset_x in range(3):
        for offset_y in range(3):
            grad_latent = (
                grad_latent
                + weights[offset_x * 3 + offset_y]
                * padded_grad[2 - offset_x : 2 - offset_x + width_x, 2 - offset_y : 2 - offset_y + width_y]
            )
    gradient = grad_latent + jnp.mean(latent, axis=0)
    return (gradient, residual_mean)


def solution(mesh):
    shape = mesh.devices.shape
    view = jax.sharding.Mesh(
        mesh.devices.reshape(shape[0] // 2, 2, shape[1]), ("vh", "vc", "star")
    )
    placed = (
        P(VOX, "star", None),
        P(None, VOX, "star", None),
        P(),
        P(),
        P(),
        P((*VOX, "star"), None, None),
        P((*VOX, "star")),
        P((*VOX, "star"), None),
        P((*VOX, "star")),
        P((*VOX, "star"), None),
        P((*VOX, "star"), None),
    )
    return jax.shard_map(
        per_device,
        mesh=view,
        in_specs=placed,
        out_specs=(P(VOX, "star", None), P((*VOX, "star"), None)),
        check_vma=False,
    )
```

```python
import jax
import jax.numpy as jnp
from jax import lax
from jax.sharding import PartitionSpec as P

HIGH = lax.Precision.HIGHEST


def exchange(cells, axis, dim, ends=None):
    count = lax.psum(1, axis)
    size = cells.shape[dim]
    if ends is None:
        head = lax.slice_in_dim(cells, 0, 1, axis=dim)
        tail = lax.slice_in_dim(cells, size - 1, size, axis=dim)
    else:
        head, tail = ends
    if count == 2:
        index = lax.axis_index(axis)
        incoming = lax.ppermute(jnp.where(index == 0, tail, head), axis, [(0, 1), (1, 0)])
        zero = jnp.zeros_like(incoming)
        below = jnp.where(index == 1, incoming, zero)
        above = jnp.where(index == 0, incoming, zero)
    else:
        below = lax.ppermute(tail, axis, [(i, i + 1) for i in range(count - 1)])
        above = lax.ppermute(head, axis, [(i + 1, i) for i in range(count - 1)])
    return jnp.concatenate([below, cells, above], axis=dim)


VOX = ("vh", "vc")


def with_halo(cells, dim, ends=None):
    return lax.optimization_barrier(exchange(exchange(cells, VOX, dim, ends), "star", dim + 1))


def rows(table, index, axis):
    numbers = lax.GatherDimensionNumbers(
        offset_dims=tuple(d for d in range(table.ndim) if d != axis),
        collapsed_slice_dims=(axis,),
        start_index_map=(axis,),
    )
    sizes = tuple(1 if d == axis else n for d, n in enumerate(table.shape))
    return lax.gather(
        table,
        index[:, None],
        numbers,
        sizes,
        mode=lax.GatherScatterMode.PROMISE_IN_BOUNDS,
    )


def per_device(
    mean_field,
    deviations,
    stencil,
    vertical_mix,
    log_mean,
    responses,
    pair_line,
    pair_owner,
    pair_star,
    observed,
    inv_var,
):
    samples = deviations.shape[0]
    width_x = deviations.shape[1]
    width_y = deviations.shape[2]
    length = deviations.shape[3]
    group_size = lax.psum(1, VOX)
    star_count = observed.shape[0]
    group_blocks = group_size * star_count
    latent = mean_field[None] + deviations
    weights = lax.optimization_barrier(
        jnp.broadcast_to(stencil.reshape(9, 1), (9, length))
    )
    ends = [
        jnp.einsum(
            "sxyw,zw->sxyz",
            mean_field[None, at : at + 1] + deviations[:, at : at + 1],
            vertical_mix,
            precision=HIGH,
        )
        for at in (0, width_x - 1)
    ]
    mixed = jnp.einsum("sxyw,zw->sxyz", latent, vertical_mix, precision=HIGH)
    padded = with_halo(mixed, 1, ends)
    smoothed = jnp.zeros(latent.shape, jnp.float32)
    for offset_x in range(3):
        for offset_y in range(3):
            smoothed = (
                smoothed
                + weights[offset_x * 3 + offset_y]
                * padded[:, offset_x : offset_x + width_x, offset_y : offset_y + width_y]
            )
    log_density = smoothed + log_mean
    density = jnp.exp(log_density)
    density_b = density.astype(jnp.bfloat16).reshape(samples, width_x * width_y, length)
    line_onehot = (
        pair_line[:, None] == jnp.arange(width_x * width_y, dtype=jnp.int32)[None, :]
    ).astype(jnp.float32)
    picked = jnp.einsum(
        "pl,slz->psz", line_onehot.astype(jnp.bfloat16), density_b, preferred_element_type=jnp.float32
    ).astype(jnp.bfloat16)
    contribution = jnp.einsum("pij,psj->psi", responses, picked, preferred_element_type=jnp.float32)
    target = pair_owner[:, 0] * star_count + pair_star
    target_onehot = (
        target[:, None] == jnp.arange(group_blocks, dtype=jnp.int32)[None, :]
    ).astype(jnp.float32)
    partial = jnp.einsum("pb,psi->bsi", target_onehot, contribution, precision=HIGH)
    pair_size = lax.psum(1, "vc")
    core = lax.axis_index("vc")
    halves = partial.reshape(group_size // pair_size, pair_size, star_count, samples, length)
    keep = lax.dynamic_index_in_dim(halves, core, axis=1, keepdims=False)
    send = lax.dynamic_index_in_dim(halves, 1 - core, axis=1, keepdims=False)
    merged = keep + lax.ppermute(send, "vc", [(0, 1), (1, 0)])
    arrived = lax.all_to_all(merged, "vh", split_axis=0, concat_axis=0, tiled=True)
    extinction = jnp.sum(arrived, axis=0)
    misfit = inv_var[:, None, :] * (extinction - observed[:, None, :])
    residual_mean = jnp.mean(misfit, axis=1)
    misfit_b = misfit.astype(jnp.bfloat16)
    spread = jnp.broadcast_to(misfit_b[None], (group_size,) + misfit_b.shape)
    misfit_b = lax.all_to_all(spread, VOX, split_axis=0, concat_axis=0, tiled=True).reshape(
        group_blocks, samples, length
    )
    pair_misfit = jnp.einsum(
        "pb,bsi->psi", target_onehot.astype(jnp.bfloat16), misfit_b, preferred_element_type=jnp.float32
    ).astype(jnp.bfloat16)
    pair_adjoint = jnp.einsum(
        "pij,psi->psj", responses, pair_misfit, preferred_element_type=jnp.float32
    )
    adjoint = jnp.einsum("pb,psj->sbj", line_onehot, pair_adjoint, precision=HIGH).reshape(
        samples, width_x, width_y, length
    )
    grad_log = jnp.mean(density * adjoint, axis=0)
    grad_smooth = jnp.einsum("xyz,zw->xyw", grad_log, vertical_mix, precision=HIGH)
    padded_grad = with_halo(grad_smooth, 0)
    grad_latent = jnp.zeros(grad_smooth.shape, jnp.float32)
    for offset_x in range(3):
        for offset_y in range(3):
            grad_latent = (
                grad_latent
                + weights[offset_x * 3 + offset_y]
                * padded_grad[2 - offset_x : 2 - offset_x + width_x, 2 - offset_y : 2 - offset_y + width_y]
            )
    gradient = grad_latent + jnp.mean(latent, axis=0)
    return (gradient, residual_mean)


def solution(mesh):
    shape = mesh.devices.shape
    view = jax.sharding.Mesh(
        mesh.devices.reshape(shape[0] // 2, 2, shape[1]), ("vh", "vc", "star")
    )
    placed = (
        P(VOX, "star", None),
        P(None, VOX, "star", None),
        P(),
        P(),
        P(),
        P((*VOX, "star"), None, None),
        P((*VOX, "star")),
        P((*VOX, "star"), None),
        P((*VOX, "star")),
        P((*VOX, "star"), None),
        P((*VOX, "star"), None),
    )
    return jax.shard_map(
        per_device,
        mesh=view,
        in_specs=placed,
        out_specs=(P(VOX, "star", None), P((*VOX, "star"), None)),
        check_vma=False,
    )
```

```python
import jax
import jax.numpy as jnp
from jax import lax
from jax.sharding import PartitionSpec as P

HIGH = lax.Precision.HIGHEST


def exchange(cells, axis, dim, ends=None):
    count = lax.psum(1, axis)
    size = cells.shape[dim]
    if ends is None:
        head = lax.slice_in_dim(cells, 0, 1, axis=dim)
        tail = lax.slice_in_dim(cells, size - 1, size, axis=dim)
    else:
        head, tail = ends
    if count == 2:
        index = lax.axis_index(axis)
        incoming = lax.ppermute(jnp.where(index == 0, tail, head), axis, [(0, 1), (1, 0)])
        zero = jnp.zeros_like(incoming)
        below = jnp.where(index == 1, incoming, zero)
        above = jnp.where(index == 0, incoming, zero)
    else:
        below = lax.ppermute(tail, axis, [(i, i + 1) for i in range(count - 1)])
        above = lax.ppermute(head, axis, [(i + 1, i) for i in range(count - 1)])
    return jnp.concatenate([below, cells, above], axis=dim)


VOX = ("vh", "vc")


def with_halo(cells, dim, ends=None):
    return lax.optimization_barrier(exchange(exchange(cells, VOX, dim, ends), "star", dim + 1))


def rows(table, index, axis):
    numbers = lax.GatherDimensionNumbers(
        offset_dims=tuple(d for d in range(table.ndim) if d != axis),
        collapsed_slice_dims=(axis,),
        start_index_map=(axis,),
    )
    sizes = tuple(1 if d == axis else n for d, n in enumerate(table.shape))
    return lax.gather(
        table,
        index[:, None],
        numbers,
        sizes,
        mode=lax.GatherScatterMode.PROMISE_IN_BOUNDS,
    )


def per_device(
    mean_field,
    deviations,
    stencil,
    vertical_mix,
    log_mean,
    responses,
    pair_line,
    pair_owner,
    pair_star,
    observed,
    inv_var,
):
    samples = deviations.shape[0]
    width_x = deviations.shape[1]
    width_y = deviations.shape[2]
    length = deviations.shape[3]
    group_size = lax.psum(1, VOX)
    star_count = observed.shape[0]
    group_blocks = group_size * star_count
    latent = mean_field[None] + deviations
    weights = lax.optimization_barrier(
        jnp.broadcast_to(stencil.reshape(9, 1), (9, length))
    )
    mixed = jnp.einsum("sxyw,zw->sxyz", latent, vertical_mix, precision=HIGH)
    padded = with_halo(mixed, 1)
    smoothed = jnp.zeros(latent.shape, jnp.float32)
    for offset_x in range(3):
        for offset_y in range(3):
            smoothed = (
                smoothed
                + weights[offset_x * 3 + offset_y]
                * padded[:, offset_x : offset_x + width_x, offset_y : offset_y + width_y]
            )
    log_density = smoothed + log_mean
    density = jnp.exp(log_density)
    density_b = density.astype(jnp.bfloat16).reshape(samples, width_x * width_y, length)
    line_onehot = (
        pair_line[:, None] == jnp.arange(width_x * width_y, dtype=jnp.int32)[None, :]
    ).astype(jnp.float32)
    picked = jnp.einsum(
        "pl,slz->psz", line_onehot.astype(jnp.bfloat16), density_b, preferred_element_type=jnp.float32
    ).astype(jnp.bfloat16)
    contribution = jnp.einsum("pij,psj->psi", responses, picked, preferred_element_type=jnp.float32)
    target = pair_owner[:, 0] * star_count + pair_star
    target_onehot = (
        target[:, None] == jnp.arange(group_blocks, dtype=jnp.int32)[None, :]
    ).astype(jnp.float32)
    partial = jnp.einsum("pb,psi->bsi", target_onehot, contribution, precision=HIGH)
    pair_size = lax.psum(1, "vc")
    core = lax.axis_index("vc")
    halves = partial.reshape(group_size // pair_size, pair_size, star_count, samples, length)
    keep = lax.dynamic_index_in_dim(halves, core, axis=1, keepdims=False)
    send = lax.dynamic_index_in_dim(halves, 1 - core, axis=1, keepdims=False)
    merged = keep + lax.ppermute(send, "vc", [(0, 1), (1, 0)])
    arrived = lax.all_to_all(merged, "vh", split_axis=0, concat_axis=0, tiled=True)
    extinction = jnp.sum(arrived, axis=0)
    misfit = inv_var[:, None, :] * (extinction - observed[:, None, :])
    residual_mean = jnp.mean(misfit, axis=1)
    misfit_b = misfit.astype(jnp.bfloat16)
    spread = jnp.broadcast_to(misfit_b[None], (group_size,) + misfit_b.shape)
    misfit_b = lax.all_to_all(spread, VOX, split_axis=0, concat_axis=0, tiled=True).reshape(
        group_blocks, samples, length
    )
    pair_misfit = jnp.einsum(
        "pb,bsi->psi", target_onehot.astype(jnp.bfloat16), misfit_b, preferred_element_type=jnp.float32
    ).astype(jnp.bfloat16)
    pair_adjoint = jnp.einsum(
        "pij,psi->psj", responses, pair_misfit, preferred_element_type=jnp.float32
    )
    adjoint = jnp.einsum("pb,psj->sbj", line_onehot, pair_adjoint, precision=HIGH).reshape(
        samples, width_x, width_y, length
    )
    grad_log = jnp.mean(density * adjoint, axis=0)
    grad_smooth = jnp.einsum("xyz,zw->xyw", grad_log, vertical_mix, precision=HIGH)
    padded_grad = with_halo(grad_smooth, 0)
    grad_latent = jnp.zeros(grad_smooth.shape, jnp.float32)
    for offset_x in range(3):
        for offset_y in range(3):
            grad_latent = (
                grad_latent
                + weights[offset_x * 3 + offset_y]
                * padded_grad[2 - offset_x : 2 - offset_x + width_x, 2 - offset_y : 2 - offset_y + width_y]
            )
    gradient = grad_latent + jnp.mean(latent, axis=0)
    return (gradient, residual_mean)


def solution(mesh):
    shape = mesh.devices.shape
    view = jax.sharding.Mesh(
        mesh.devices.reshape(shape[0] // 2, 2, shape[1]), ("vh", "vc", "star")
    )
    placed = (
        P(VOX, "star", None),
        P(None, VOX, "star", None),
        P(),
        P(),
        P(),
        P((*VOX, "star"), None, None),
        P((*VOX, "star")),
        P((*VOX, "star"), None),
        P((*VOX, "star")),
        P((*VOX, "star"), None),
        P((*VOX, "star"), None),
    )
    return jax.shard_map(
        per_device,
        mesh=view,
        in_specs=placed,
        out_specs=(P(VOX, "star", None), P((*VOX, "star"), None)),
        check_vma=False,
    )
```

```python
import jax
import jax.numpy as jnp
from jax import lax
from jax.sharding import PartitionSpec as P

HIGH = lax.Precision.HIGHEST


def exchange(cells, axis, dim):
    count = lax.psum(1, axis)
    size = cells.shape[dim]
    head = lax.slice_in_dim(cells, 0, 1, axis=dim)
    tail = lax.slice_in_dim(cells, size - 1, size, axis=dim)
    if count == 2:
        index = lax.axis_index(axis)
        both = lax.ppermute(jnp.concatenate([head, tail], axis=dim), axis, [(0, 1), (1, 0)])
        zero = jnp.zeros_like(head)
        below = jnp.where(index == 1, lax.slice_in_dim(both, 1, 2, axis=dim), zero)
        above = jnp.where(index == 0, lax.slice_in_dim(both, 0, 1, axis=dim), zero)
    else:
        below = lax.ppermute(tail, axis, [(i, i + 1) for i in range(count - 1)])
        above = lax.ppermute(head, axis, [(i + 1, i) for i in range(count - 1)])
    return jnp.concatenate([below, cells, above], axis=dim)


VOX = ("vh", "vc")


def with_halo(cells, dim):
    return lax.optimization_barrier(exchange(exchange(cells, VOX, dim), "star", dim + 1))


def rows(table, index, axis):
    numbers = lax.GatherDimensionNumbers(
        offset_dims=tuple(d for d in range(table.ndim) if d != axis),
        collapsed_slice_dims=(axis,),
        start_index_map=(axis,),
    )
    sizes = tuple(1 if d == axis else n for d, n in enumerate(table.shape))
    return lax.gather(
        table,
        index[:, None],
        numbers,
        sizes,
        mode=lax.GatherScatterMode.PROMISE_IN_BOUNDS,
    )


def per_device(
    mean_field,
    deviations,
    stencil,
    vertical_mix,
    log_mean,
    responses,
    pair_line,
    pair_owner,
    pair_star,
    observed,
    inv_var,
):
    samples = deviations.shape[0]
    width_x = deviations.shape[1]
    width_y = deviations.shape[2]
    length = deviations.shape[3]
    group_size = lax.psum(1, VOX)
    star_count = observed.shape[0]
    group_blocks = group_size * star_count
    latent = mean_field[None] + deviations
    weights = lax.optimization_barrier(
        jnp.broadcast_to(stencil.reshape(9, 1), (9, length))
    )
    padded = with_halo(latent, 1)
    smoothed = jnp.zeros(latent.shape, jnp.float32)
    for offset_x in range(3):
        for offset_y in range(3):
            smoothed = (
                smoothed
                + weights[offset_x * 3 + offset_y]
                * padded[:, offset_x : offset_x + width_x, offset_y : offset_y + width_y]
            )
    log_density = jnp.einsum("sxyw,zw->sxyz", smoothed, vertical_mix, precision=HIGH) + log_mean
    density = jnp.exp(log_density)
    density_b = density.astype(jnp.bfloat16).reshape(samples, width_x * width_y, length)
    line_onehot = (
        pair_line[:, None] == jnp.arange(width_x * width_y, dtype=jnp.int32)[None, :]
    ).astype(jnp.float32)
    picked = jnp.einsum(
        "pl,slz->psz", line_onehot.astype(jnp.bfloat16), density_b, preferred_element_type=jnp.float32
    ).astype(jnp.bfloat16)
    contribution = jnp.einsum("pij,psj->psi", responses, picked, preferred_element_type=jnp.float32)
    target = pair_owner[:, 0] * star_count + pair_star
    target_onehot = (
        target[:, None] == jnp.arange(group_blocks, dtype=jnp.int32)[None, :]
    ).astype(jnp.float32)
    partial = jnp.einsum("pb,psi->bsi", target_onehot, contribution, precision=HIGH)
    pair_size = lax.psum(1, "vc")
    core = lax.axis_index("vc")
    halves = partial.reshape(group_size // pair_size, pair_size, star_count, samples, length)
    keep = lax.dynamic_index_in_dim(halves, core, axis=1, keepdims=False)
    send = lax.dynamic_index_in_dim(halves, 1 - core, axis=1, keepdims=False)
    merged = keep + lax.ppermute(send, "vc", [(0, 1), (1, 0)])
    arrived = lax.all_to_all(merged, "vh", split_axis=0, concat_axis=0, tiled=True)
    extinction = jnp.sum(arrived, axis=0)
    misfit = inv_var[:, None, :] * (extinction - observed[:, None, :])
    residual_mean = jnp.mean(misfit, axis=1)
    misfit_b = misfit.astype(jnp.bfloat16)
    spread = jnp.broadcast_to(misfit_b[None], (group_size,) + misfit_b.shape)
    misfit_b = lax.all_to_all(spread, VOX, split_axis=0, concat_axis=0, tiled=True).reshape(
        group_blocks, samples, length
    )
    pair_misfit = jnp.einsum(
        "pb,bsi->psi", target_onehot.astype(jnp.bfloat16), misfit_b, preferred_element_type=jnp.float32
    ).astype(jnp.bfloat16)
    pair_adjoint = jnp.einsum(
        "pij,psi->psj", responses, pair_misfit, preferred_element_type=jnp.float32
    )
    adjoint = jnp.einsum("pb,psj->sbj", line_onehot, pair_adjoint, precision=HIGH).reshape(
        samples, width_x, width_y, length
    )
    grad_log = jnp.mean(density * adjoint, axis=0)
    grad_smooth = jnp.einsum("xyz,zw->xyw", grad_log, vertical_mix, precision=HIGH)
    padded_grad = with_halo(grad_smooth, 0)
    grad_latent = jnp.zeros(grad_smooth.shape, jnp.float32)
    for offset_x in range(3):
        for offset_y in range(3):
            grad_latent = (
                grad_latent
                + weights[offset_x * 3 + offset_y]
                * padded_grad[2 - offset_x : 2 - offset_x + width_x, 2 - offset_y : 2 - offset_y + width_y]
            )
    gradient = grad_latent + jnp.mean(latent, axis=0)
    return (gradient, residual_mean)


def solution(mesh):
    shape = mesh.devices.shape
    view = jax.sharding.Mesh(
        mesh.devices.reshape(shape[0] // 2, 2, shape[1]), ("vh", "vc", "star")
    )
    placed = (
        P(VOX, "star", None),
        P(None, VOX, "star", None),
        P(),
        P(),
        P(),
        P((*VOX, "star"), None, None),
        P((*VOX, "star")),
        P((*VOX, "star"), None),
        P((*VOX, "star")),
        P((*VOX, "star"), None),
        P((*VOX, "star"), None),
    )
    return jax.shard_map(
        per_device,
        mesh=view,
        in_specs=placed,
        out_specs=(P(VOX, "star", None), P((*VOX, "star"), None)),
        check_vma=False,
    )
```

```python
import jax
import jax.numpy as jnp
from jax import lax
from jax.sharding import PartitionSpec as P

HIGH = lax.Precision.HIGHEST


def exchange(cells, axis, dim):
    count = lax.psum(1, axis)
    size = cells.shape[dim]
    head = lax.slice_in_dim(cells, 0, 1, axis=dim)
    tail = lax.slice_in_dim(cells, size - 1, size, axis=dim)
    if count == 2:
        index = lax.axis_index(axis)
        incoming = lax.ppermute(jnp.where(index == 0, tail, head), axis, [(0, 1), (1, 0)])
        zero = jnp.zeros_like(incoming)
        below = jnp.where(index == 1, incoming, zero)
        above = jnp.where(index == 0, incoming, zero)
    else:
        below = lax.ppermute(tail, axis, [(i, i + 1) for i in range(count - 1)])
        above = lax.ppermute(head, axis, [(i + 1, i) for i in range(count - 1)])
    return jnp.concatenate([below, cells, above], axis=dim)


VOX = ("vh", "vc")


def with_halo(cells, dim):
    return lax.optimization_barrier(exchange(exchange(cells, VOX, dim), "star", dim + 1))


def rows(table, index, axis):
    numbers = lax.GatherDimensionNumbers(
        offset_dims=tuple(d for d in range(table.ndim) if d != axis),
        collapsed_slice_dims=(axis,),
        start_index_map=(axis,),
    )
    sizes = tuple(1 if d == axis else n for d, n in enumerate(table.shape))
    return lax.gather(
        table,
        index[:, None],
        numbers,
        sizes,
        mode=lax.GatherScatterMode.PROMISE_IN_BOUNDS,
    )


def per_device(
    mean_field,
    deviations,
    stencil,
    vertical_mix,
    log_mean,
    responses,
    pair_line,
    pair_owner,
    pair_star,
    observed,
    inv_var,
):
    samples = deviations.shape[0]
    width_x = deviations.shape[1]
    width_y = deviations.shape[2]
    length = deviations.shape[3]
    group_size = lax.psum(1, VOX)
    star_count = observed.shape[0]
    group_blocks = group_size * star_count
    latent = mean_field[None] + deviations
    weights = lax.optimization_barrier(
        jnp.broadcast_to(stencil.reshape(9, 1), (9, length))
    )
    padded = with_halo(latent, 1)
    smoothed = jnp.zeros(latent.shape, jnp.float32)
    for offset_x in range(3):
        for offset_y in range(3):
            smoothed = (
                smoothed
                + weights[offset_x * 3 + offset_y]
                * padded[:, offset_x : offset_x + width_x, offset_y : offset_y + width_y]
            )
    log_density = jnp.einsum("sxyw,zw->sxyz", smoothed, vertical_mix, precision=HIGH) + log_mean
    density = jnp.exp(log_density)
    density_b = density.astype(jnp.bfloat16).reshape(samples, width_x * width_y, length)
    line_onehot = (
        pair_line[:, None] == jnp.arange(width_x * width_y, dtype=jnp.int32)[None, :]
    ).astype(jnp.float32)
    picked = jnp.einsum(
        "pl,slz->psz", line_onehot.astype(jnp.bfloat16), density_b, preferred_element_type=jnp.float32
    ).astype(jnp.bfloat16)
    contribution = jnp.einsum("pij,psj->psi", responses, picked, preferred_element_type=jnp.float32)
    target = pair_owner[:, 0] * star_count + pair_star
    target_onehot = (
        target[:, None] == jnp.arange(group_blocks, dtype=jnp.int32)[None, :]
    ).astype(jnp.float32)
    partial = jnp.einsum("pb,psi->bsi", target_onehot, contribution, precision=HIGH)
    pair_size = lax.psum(1, "vc")
    core = lax.axis_index("vc")
    halves = partial.reshape(group_size // pair_size, pair_size, star_count, samples, length)
    keep = lax.dynamic_index_in_dim(halves, core, axis=1, keepdims=False)
    send = lax.dynamic_index_in_dim(halves, 1 - core, axis=1, keepdims=False)
    merged = keep + lax.ppermute(send, "vc", [(0, 1), (1, 0)])
    arrived = lax.all_to_all(merged, "vh", split_axis=0, concat_axis=0, tiled=True)
    extinction = jnp.sum(arrived, axis=0)
    misfit = inv_var[:, None, :] * (extinction - observed[:, None, :])
    residual_mean = jnp.mean(misfit, axis=1)
    misfit_b = misfit.astype(jnp.bfloat16)
    spread = jnp.broadcast_to(misfit_b[None], (group_size,) + misfit_b.shape)
    misfit_b = lax.all_to_all(spread, VOX, split_axis=0, concat_axis=0, tiled=True).reshape(
        group_blocks, samples, length
    )
    pair_misfit = jnp.einsum(
        "pb,bsi->psi", target_onehot.astype(jnp.bfloat16), misfit_b, preferred_element_type=jnp.float32
    ).astype(jnp.bfloat16)
    pair_adjoint = jnp.einsum(
        "pij,psi->psj", responses, pair_misfit, preferred_element_type=jnp.float32
    )
    adjoint = (
        jnp.zeros((width_x * width_y, samples, length), jnp.float32)
        .at[pair_line]
        .add(pair_adjoint, mode="promise_in_bounds")
        .transpose(1, 0, 2)
        .reshape(samples, width_x, width_y, length)
    )
    grad_log = jnp.mean(density * adjoint, axis=0)
    grad_smooth = jnp.einsum("xyz,zw->xyw", grad_log, vertical_mix, precision=HIGH)
    padded_grad = with_halo(grad_smooth, 0)
    grad_latent = jnp.zeros(grad_smooth.shape, jnp.float32)
    for offset_x in range(3):
        for offset_y in range(3):
            grad_latent = (
                grad_latent
                + weights[offset_x * 3 + offset_y]
                * padded_grad[2 - offset_x : 2 - offset_x + width_x, 2 - offset_y : 2 - offset_y + width_y]
            )
    gradient = grad_latent + jnp.mean(latent, axis=0)
    return (gradient, residual_mean)


def solution(mesh):
    shape = mesh.devices.shape
    view = jax.sharding.Mesh(
        mesh.devices.reshape(shape[0] // 2, 2, shape[1]), ("vh", "vc", "star")
    )
    placed = (
        P(VOX, "star", None),
        P(None, VOX, "star", None),
        P(),
        P(),
        P(),
        P((*VOX, "star"), None, None),
        P((*VOX, "star")),
        P((*VOX, "star"), None),
        P((*VOX, "star")),
        P((*VOX, "star"), None),
        P((*VOX, "star"), None),
    )
    return jax.shard_map(
        per_device,
        mesh=view,
        in_specs=placed,
        out_specs=(P(VOX, "star", None), P((*VOX, "star"), None)),
        check_vma=False,
    )
```
